32 devices in a mesh: section: 2 (over x), mp: 4 (over z), dp: 4 (over y, core).
Axes of the slice: x: 2, y: 2, z: 4, core: 2. Of those that a mesh axis runs over, the one named last changes fastest.
Arguments:
- text_in: bfloat16 [4, 2, 512, 8192], P('dp', 'section', None, 'mp'), may hold values from -6 to 6
- vision: bfloat16 [4, 2, 256, 8192], P('dp', 'section', None, 'mp'), may hold values from -6 to 6
- tile_counts: int32 [4, 2], P('dp'), may hold values from 1 to 4, as said below
- lengths: int32 [4, 2], P('dp', 'section'), may hold values from 128 to 512, as said below
- image_of: int32 [4, 2], P('dp'), may hold values from 0 to 1, each once within a row
- norm_gain: float32 [2, 8192], P('section'), may hold values from 0.5 to 1.5
- query_weight: bfloat16 [2, 8192, 4096], P('section', 'dp', 'mp'), may hold values from -0.0625 to 0.0625
- key_weight: bfloat16 [2, 8192, 1024], P('section', 'dp', 'mp'), may hold values from -0.0625 to 0.0625
- value_weight: bfloat16 [2, 8192, 1024], P('section', 'dp', 'mp'), may hold values from -0.0625 to 0.0625
- query_gain: float32 [2, 128], P('section')
- key_gain: float32 [2, 128], P('section')
- cross_gate: float32 [2], P('section'), may hold values from 0.4 to 1.5
- context_grad: bfloat16 [4, 2, 512, 4096], P('dp', 'section', None, 'mp'), may hold values from -6 to 6
Outputs:
- gated_context: bfloat16 [4, 2, 512, 4096], P('dp', 'section', None, 'mp')
- vision_grad: bfloat16 [4, 2, 256, 8192], P('dp', 'section', None, 'mp')
- key_weight_grad: bfloat16 [2, 8192, 1024], P('section', 'dp', 'mp')
- value_weight_grad: bfloat16 [2, 8192, 1024], P('section', 'dp', 'mp')
The draws below stay inside these ranges and needn't reach their ends.
Inputs may be any that keep to these rules, and one draw needn't show every extreme that they name: `tile_counts`: some image has 4 tiles and some has one. `lengths`: some sample has the full 512 tokens. `image_of`: each row is a permutation of the sections.
All inputs are finite; a program needn't handle non-finite values.
Results may differ from the reference program's by a relative error of at most 0.018.
Values may be sent and summed in bfloat16 or wider, within the bound.
No kernel may reach another device: no remote copies, remote signals or barrier semaphores. Data moves between devices by JAX's collectives and lax.ppermute only.
A program may use at most 192 MiB of HBM per device.

```python
import jax
import jax.numpy as jnp
from jax import lax

D = 8192
QH = 32
KVH = 8
HD = 128
TXT = 512
TILE_ROWS = 64
MAX_TILES = 4
VROWS = 256
SECTIONS = 2
SAMPLES = 4
N_MP = 4


def draw_tile_counts(key, part):
    counts = jax.random.randint(key, (SAMPLES, SECTIONS), 1, MAX_TILES + 1)
    counts = counts.at[0, 0].set(MAX_TILES)
    return counts.at[0, 1].set(1).astype(jnp.int32)


def draw_lengths(key, part):
    counts = jax.random.randint(key, (SAMPLES, SECTIONS), TXT // 4, TXT + 1)
    return counts.at[0, 0].set(TXT).astype(jnp.int32)


def draw_query_gain(key, part):
    base = jax.random.uniform(jax.random.fold_in(key, 11), (SECTIONS, HD), jnp.float32, 0.5, 1.5)
    return base


def draw_key_gain(key, part):
    base = jax.random.uniform(jax.random.fold_in(key, 13), (SECTIONS, HD), jnp.float32, 0.5, 1.5)
    return base


def level_of(stream_key, extent, pieces, smallest, top_value):
    factor_of = 1.0
    for position, parts in pieces:
        draws = jax.random.uniform(jax.random.fold_in(jax.random.fold_in(stream_key, 6), position), (parts,), jnp.float32, smallest / len(pieces), top_value / len(pieces))
        factor_of = factor_of * jnp.repeat(jnp.exp(draws), extent[position] // parts).reshape((-1,) + (1,) * (len(extent) - 1 - position))
    return factor_of


def normal_values(stream_key, dims, scale, limit, split=(), kind=jnp.bfloat16):
    result = jax.random.normal(stream_key, dims, jnp.float32) * scale
    if len(split) > 0:
        result = level_of(stream_key, dims, split, -0.22, 0.18) * result
    return jnp.clip(result, min=-limit, max=limit).astype(kind)


def setup_inputs(seed: int = 0) -> dict:
    key_list = jax.random.split(jax.random.key(seed), 14)
    return {
        "text_in": normal_values(key_list[0], (SAMPLES, SECTIONS, TXT, D), 1.0, 6.0, ((0, 4), (1, 2), (3, 4))),
        "vision": normal_values(key_list[1], (SAMPLES, SECTIONS, VROWS, D), 1.0, 6.0, ((0, 4), (1, 2), (3, 4))),
        "tile_counts": draw_tile_counts(jax.random.fold_in(key_list[13], 71), 0),
        "lengths": draw_lengths(jax.random.fold_in(key_list[13], 71), 0),
        "image_of": jax.vmap(lambda own: jax.random.permutation(own, SECTIONS))(jax.random.split(key_list[4], SAMPLES)).reshape((SAMPLES, SECTIONS)).astype(jnp.int32),
        "norm_gain": jnp.clip(1.0 + 0.1 * jax.random.normal(key_list[5], (SECTIONS, D), jnp.float32), 0.5, 1.5),
        "query_weight": normal_values(key_list[6], (SECTIONS, D, QH * HD), D ** -0.5, 0.0625, ((0, 2), (1, 4), (2, 4))),
        "key_weight": normal_values(key_list[7], (SECTIONS, D, KVH * HD), D ** -0.5, 0.0625, ((0, 2), (1, 4), (2, 4))),
        "value_weight": normal_values(key_list[8], (SECTIONS, D, KVH * HD), D ** -0.5, 0.0625, ((0, 2), (1, 4), (2, 4))),
        "query_gain": draw_query_gain(jax.random.fold_in(key_list[13], 71), 0),
        "key_gain": draw_key_gain(jax.random.fold_in(key_list[13], 71), 0),
        "cross_gate": jnp.clip(0.4 + 1.1 * jax.random.uniform(key_list[11], (SECTIONS,), jnp.float32) ** level_of(key_list[11], (SECTIONS,), ((0, 2),), -0.2, 0.2), 0.4, 1.5),
        "context_grad": normal_values(key_list[12], (SAMPLES, SECTIONS, TXT, QH * HD), 1.0, 6.0, ((0, 4), (1, 2), (3, 4))),
    }


def norm_rows(values, gain):
    values = values.astype(jnp.float32)
    scaled = values * lax.rsqrt(lax.optimization_barrier(jnp.mean(values * values, axis=-1, keepdims=True)) + 1e-05)
    return scaled * gain.astype(jnp.float32)

def rounded(values):
    return lax.optimization_barrier(values.astype(jnp.bfloat16)).astype(jnp.float32)

def attend(queries, keys_raw, values_raw, key_norm, usable, present, gate_value):
    keys = rounded(norm_rows(keys_raw, key_norm))
    values = rounded(values_raw)
    text_rows, heads, depth = queries.shape
    groups = keys.shape[1]
    grouped = queries.astype(jnp.float32).reshape(text_rows, groups, heads // groups, depth)
    scores = jnp.einsum('tgjd,vgd->gjtv', grouped, keys) * depth ** (-0.5)
    scores = jnp.where(usable[None, None, None, :], scores, -1e+30)
    highest = lax.stop_gradient(lax.optimization_barrier(jnp.max(scores, axis=-1, keepdims=True)))
    weights = jnp.exp(scores - highest)
    probs = rounded(weights / lax.optimization_barrier(jnp.sum(weights, axis=-1, keepdims=True)))
    context = jnp.einsum('gjtv,vgd->tgjd', probs, values).reshape(text_rows, heads * depth)
    return jnp.where(present[:, None], jnp.tanh(gate_value) * context, 0.0)

def one_section(section_id, text_in, vision, tile_counts, lengths, image_of, norm_gain, query_weight, key_weight, value_weight, query_gain, key_gain, cross_gate, context_grad):
    wq = query_weight[section_id]
    wk = key_weight[section_id]
    wv = value_weight[section_id]
    key_width = wk.shape[1]
    group_width = key_width // N_MP
    contexts = []
    image_grads = []
    key_total = jnp.zeros((D, key_width), jnp.float32)
    value_total = jnp.zeros((D, key_width), jnp.float32)
    for sample in range(SAMPLES):
        text = text_in[sample, (section_id - 1) % SECTIONS]
        owner = image_of[sample, section_id]
        image = vision[sample, owner]
        normed = norm_rows(text, norm_gain[section_id]).astype(jnp.bfloat16)
        query_raw = jnp.dot(normed, wq, preferred_element_type=jnp.float32)
        queries = norm_rows(query_raw.reshape(TXT, QH, HD), query_gain[section_id]).astype(jnp.bfloat16)
        keys_raw = jnp.dot(image, wk, preferred_element_type=jnp.float32).reshape(VROWS, KVH, HD)
        values_raw = jnp.dot(image, wv, preferred_element_type=jnp.float32).reshape(VROWS, KVH, HD)
        usable = jnp.arange(VROWS) < tile_counts[sample, owner] * TILE_ROWS
        present = jnp.arange(TXT) < lengths[sample, section_id]

        def forward(keys_in, values_in):
            return attend(queries, keys_in, values_in, key_gain[section_id], usable, present, cross_gate[section_id])
        context, pullback = jax.vjp(forward, keys_raw, values_raw)
        contexts.append(context.astype(jnp.bfloat16))
        key_cot, value_cot = pullback(context_grad[sample, section_id].astype(jnp.float32))
        key_flat = key_cot.reshape(VROWS, key_width).astype(jnp.bfloat16)
        value_flat = value_cot.reshape(VROWS, key_width).astype(jnp.bfloat16)
        term_k = jnp.einsum('vjc,djc->jvd', key_flat.astype(jnp.float32).reshape(VROWS, N_MP, group_width), wk.astype(jnp.float32).reshape(D, N_MP, group_width))
        term_v = jnp.einsum('vjc,djc->jvd', value_flat.astype(jnp.float32).reshape(VROWS, N_MP, group_width), wv.astype(jnp.float32).reshape(D, N_MP, group_width))
        terms = (term_k + term_v).astype(jnp.bfloat16).astype(jnp.float32)
        image_grads.append(lax.optimization_barrier(jnp.sum(terms, axis=0)).astype(jnp.bfloat16))
        key_part = jnp.dot(image.T, key_flat, preferred_element_type=jnp.float32).astype(jnp.bfloat16)
        value_part = jnp.dot(image.T, value_flat, preferred_element_type=jnp.float32).astype(jnp.bfloat16)
        key_total = key_total + key_part.astype(jnp.float32)
        value_total = value_total + value_part.astype(jnp.float32)
    return (jnp.stack(contexts), jnp.stack(image_grads), key_total.astype(jnp.bfloat16), value_total.astype(jnp.bfloat16))

def reference(text_in, vision, tile_counts, lengths, image_of, norm_gain, query_weight, key_weight, value_weight, query_gain, key_gain, cross_gate, context_grad):

    def per_section(section_id):
        return one_section(section_id, text_in, vision, tile_counts, lengths, image_of, norm_gain, query_weight, key_weight, value_weight, query_gain, key_gain, cross_gate, context_grad)
    contexts, image_grads, key_grads, value_grads = lax.map(per_section, jnp.arange(SECTIONS, dtype=jnp.int32))
    gated_context = jnp.swapaxes(contexts, 0, 1)
    by_sample = jnp.swapaxes(image_grads, 0, 1)
    inverse = jnp.argsort(image_of, axis=1).astype(jnp.int32)
    vision_grad = jnp.take_along_axis(by_sample, inverse[:, :, None, None], axis=1)
    return (gated_context, vision_grad, key_grads, value_grads)
```

```python
import jax
import jax.numpy as jnp
from jax import lax
from jax.sharding import PartitionSpec as P

HD = 128
TILE_ROWS = 64


def shifted(value, axis, steps):
    count = lax.axis_size(axis)
    pairs = [(source, (source + steps) % count) for source in range(count)]
    return lax.ppermute(value, axis, pairs)


def swapped(value, axis, mask):
    count = lax.axis_size(axis)
    pairs = [(source, source ^ mask) for source in range(count)]
    return lax.ppermute(value, axis, pairs)


def bit_order(count, high_first):
    bits = []
    step = 1
    while step < count:
        bits.append(step)
        step *= 2
    return bits[::-1] if high_first else bits


def gather_blocks(block, axis):
    count = lax.axis_size(axis)
    held = {0: block}
    for mask in bit_order(count, True):
        codes = sorted(held)
        arrived = swapped(jnp.stack([held[c] for c in codes]), axis, mask)
        for position, code in enumerate(codes):
            held[code ^ mask] = arrived[position]
    return held


def scatter_blocks(by_code, axis):
    count = lax.axis_size(axis)
    held = {code: value.astype(jnp.float32) for code, value in by_code.items()}
    for mask in bit_order(count, False):
        sent = sorted(c for c in held if c & mask)
        kept = [c ^ mask for c in sent]
        arrived = swapped(jnp.stack([held[c].astype(jnp.bfloat16) for c in sent]), axis, mask)
        held = {c: held[c] + arrived[position].astype(jnp.float32) for position, c in enumerate(kept)}
    return held[0]


def norm_rows(values, gain):
    values = values.astype(jnp.float32)
    scaled = values * lax.rsqrt(jnp.mean(values * values, axis=-1, keepdims=True) + 1e-05)
    return scaled * gain


def rounded(values):
    return lax.optimization_barrier(values.astype(jnp.bfloat16)).astype(jnp.float32)


def attend(queries, keys_raw, values_raw, key_norm, usable, present, gate_value):
    keys = rounded(norm_rows(keys_raw, key_norm))
    values = rounded(values_raw)
    text_rows, heads, depth = queries.shape
    groups = keys.shape[1]
    grouped = queries.astype(jnp.float32).reshape(text_rows, groups, heads // groups, depth)
    scores = jnp.einsum("tgjd,vgd->gjtv", grouped, keys) * depth ** (-0.5)
    scores = jnp.where(usable[None, None, None, :], scores, -1e30)
    highest = lax.stop_gradient(jnp.max(scores, axis=-1, keepdims=True))
    weights = jnp.exp(scores - highest)
    probs = rounded(weights / jnp.sum(weights, axis=-1, keepdims=True))
    context = jnp.einsum("gjtv,vgd->tgjd", probs, values).reshape(text_rows, heads * depth)
    return jnp.where(present[:, None], jnp.tanh(gate_value) * context, 0.0)


def columns_of(values, start, width):
    return lax.dynamic_slice_in_dim(values, start, width, axis=1)


def per_device(
    text_in,
    vision,
    tile_counts,
    lengths,
    image_of,
    norm_gain,
    query_weight,
    key_weight,
    value_weight,
    query_gain,
    key_gain,
    cross_gate,
    context_grad,
):
    sections = lax.axis_size("section")
    section = lax.axis_index("section")
    dp_index = lax.axis_index("dp")
    block_rows = query_weight.shape[1]

    query_blocks = gather_blocks(query_weight[0], "dp")
    key_blocks = gather_blocks(key_weight[0], "dp")
    value_blocks = gather_blocks(value_weight[0], "dp")

    arrived = shifted(text_in, "section", 1)
    full_text = lax.all_gather(arrived, "mp", axis=3, tiled=True)[0, 0]
    text_rows = full_text.shape[0]
    normed = norm_rows(full_text, norm_gain[0]).astype(jnp.bfloat16)
    width_q = query_weight.shape[2]
    query_raw = None
    for code, block in query_blocks.items():
        part = jnp.dot(
            columns_of(normed, (dp_index ^ code) * block_rows, block_rows),
            block,
            preferred_element_type=jnp.float32,
        )
        query_raw = part if query_raw is None else query_raw + part
    queries = norm_rows(query_raw.reshape(text_rows, width_q // HD, HD), query_gain[0]).astype(
        jnp.bfloat16
    )

    slot_rows = vision.shape[2]
    part_width = vision.shape[3]
    wanted = image_of[0, section]
    image_part = vision[0, 0]
    for steps in range(1, sections):
        moved = shifted(vision, "section", steps)[0, 0]
        image_part = jnp.where((section - steps) % sections == wanted, moved, image_part)
    image = lax.all_gather(image_part, "mp", axis=1, tiled=True)

    width_k = key_weight.shape[2]
    keys_raw = None
    values_raw = None
    for code in key_blocks:
        piece = columns_of(image, (dp_index ^ code) * block_rows, block_rows)
        key_part = jnp.dot(piece, key_blocks[code], preferred_element_type=jnp.float32)
        value_part = jnp.dot(piece, value_blocks[code], preferred_element_type=jnp.float32)
        keys_raw = key_part if keys_raw is None else keys_raw + key_part
        values_raw = value_part if values_raw is None else values_raw + value_part
    keys_raw = keys_raw.reshape(slot_rows, width_k // HD, HD)
    values_raw = values_raw.reshape(slot_rows, width_k // HD, HD)
    usable = jnp.arange(slot_rows) < tile_counts[0, wanted] * TILE_ROWS
    present = jnp.arange(text_rows) < lengths[0, 0]

    def forward(keys_in, values_in):
        return attend(queries, keys_in, values_in, key_gain[0], usable, present, cross_gate[0])

    context, pullback = jax.vjp(forward, keys_raw, values_raw)
    gated_context = context.astype(jnp.bfloat16).reshape(1, 1, text_rows, width_q)
    key_back, value_back = pullback(context_grad[0, 0].astype(jnp.float32))
    key_flat = key_back.reshape(slot_rows, width_k).astype(jnp.bfloat16)
    value_flat = value_back.reshape(slot_rows, width_k).astype(jnp.bfloat16)

    contract = (((1,), (1,)), ((), ()))
    partial_sum = jnp.zeros((slot_rows, image.shape[1]), jnp.bfloat16)
    for code in key_blocks:
        term = lax.dot_general(key_flat, key_blocks[code], contract, preferred_element_type=jnp.float32)
        term = term + lax.dot_general(
            value_flat, value_blocks[code], contract, preferred_element_type=jnp.float32
        )
        partial_sum = lax.dynamic_update_slice_in_dim(
            partial_sum, term.astype(jnp.bfloat16), (dp_index ^ code) * block_rows, axis=1
        )
    summed = lax.psum_scatter(partial_sum, "mp", scatter_dimension=1, tiled=True)

    routed = summed
    for steps in range(1, sections):
        moved = shifted(summed, "section", steps)
        source = (section - steps) % sections
        routed = jnp.where(image_of[0, source] == section, moved, routed)
    vision_grad = routed.reshape(1, 1, slot_rows, part_width)

    inner = (((0,), (0,)), ((), ()))
    grad_blocks = {}
    for code in key_blocks:
        piece = columns_of(image, (dp_index ^ code) * block_rows, block_rows)
        key_part = lax.dot_general(piece, key_flat, inner, preferred_element_type=jnp.float32)
        value_part = lax.dot_general(piece, value_flat, inner, preferred_element_type=jnp.float32)
        grad_blocks[code] = jnp.concatenate(
            [key_part.astype(jnp.bfloat16), value_part.astype(jnp.bfloat16)], axis=1
        )
    both_grads = scatter_blocks(grad_blocks, "dp").astype(jnp.bfloat16)
    key_weight_grad = both_grads[:, :width_k][None]
    value_weight_grad = both_grads[:, width_k:][None]
    return (gated_context, vision_grad, key_weight_grad, value_weight_grad)


def solution(mesh):
    return jax.shard_map(
        per_device,
        mesh=mesh,
        in_specs=(
            P("dp", "section", None, "mp"),
            P("dp", "section", None, "mp"),
            P("dp", None),
            P("dp", "section"),
            P("dp", None),
            P("section", None),
            P("section", "dp", "mp"),
            P("section", "dp", "mp"),
            P("section", "dp", "mp"),
            P("section", None),
            P("section", None),
            P("section"),
            P("dp", "section", None, "mp"),
        ),
        out_specs=(
            P("dp", "section", None, "mp"),
            P("dp", "section", None, "mp"),
            P("section", "dp", "mp"),
            P("section", "dp", "mp"),
        ),
        check_vma=False,
    )
```

```python
import jax
import jax.numpy as jnp
from jax import lax
from jax.sharding import PartitionSpec as P

HD = 128
TILE_ROWS = 64


def shifted(value, axis, steps):
    count = lax.axis_size(axis)
    pairs = [(source, (source + steps) % count) for source in range(count)]
    return lax.ppermute(value, axis, pairs)


def swapped(value, axis, mask):
    count = lax.axis_size(axis)
    pairs = [(source, source ^ mask) for source in range(count)]
    return lax.ppermute(value, axis, pairs)


def bit_order(count, high_first):
    bits = []
    step = 1
    while step < count:
        bits.append(step)
        step *= 2
    return bits[::-1] if high_first else bits


def gather_blocks(block, axis):
    count = lax.axis_size(axis)
    held = {0: block}
    for mask in bit_order(count, True):
        codes = sorted(held)
        arrived = swapped(jnp.stack([held[c] for c in codes]), axis, mask)
        for position, code in enumerate(codes):
            held[code ^ mask] = arrived[position]
    return held


def scatter_blocks(by_code, axis):
    count = lax.axis_size(axis)
    held = {code: value.astype(jnp.float32) for code, value in by_code.items()}
    for mask in bit_order(count, False):
        sent = sorted(c for c in held if c & mask)
        kept = [c ^ mask for c in sent]
        arrived = swapped(jnp.stack([held[c].astype(jnp.bfloat16) for c in sent]), axis, mask)
        held = {c: held[c] + arrived[position].astype(jnp.float32) for position, c in enumerate(kept)}
    return held[0]


def norm_rows(values, gain):
    values = values.astype(jnp.float32)
    scaled = values * lax.rsqrt(jnp.mean(values * values, axis=-1, keepdims=True) + 1e-05)
    return scaled * gain


def rounded(values):
    return lax.optimization_barrier(values.astype(jnp.bfloat16)).astype(jnp.float32)


def attend(queries, keys_raw, values_raw, key_norm, usable, present, gate_value):
    keys = rounded(norm_rows(keys_raw, key_norm))
    values = rounded(values_raw)
    text_rows, heads, depth = queries.shape
    groups = keys.shape[1]
    grouped = queries.astype(jnp.float32).reshape(text_rows, groups, heads // groups, depth)
    scores = jnp.einsum("tgjd,vgd->gjtv", grouped, keys) * depth ** (-0.5)
    scores = jnp.where(usable[None, None, None, :], scores, -1e30)
    highest = lax.stop_gradient(jnp.max(scores, axis=-1, keepdims=True))
    weights = jnp.exp(scores - highest)
    probs = rounded(weights / jnp.sum(weights, axis=-1, keepdims=True))
    context = jnp.einsum("gjtv,vgd->tgjd", probs, values).reshape(text_rows, heads * depth)
    return jnp.where(present[:, None], jnp.tanh(gate_value) * context, 0.0)


def code_columns(values, index, count, width):
    pieces = [lax.dynamic_slice_in_dim(values, (index ^ code) * width, width, axis=1) for code in range(count)]
    return jnp.concatenate(pieces, axis=1)


def stacked(held):
    return jnp.concatenate([held[code] for code in range(len(held))], axis=0)


def per_device(
    text_in,
    vision,
    tile_counts,
    lengths,
    image_of,
    norm_gain,
    query_weight,
    key_weight,
    value_weight,
    query_gain,
    key_gain,
    cross_gate,
    context_grad,
):
    sections = lax.axis_size("section")
    section = lax.axis_index("section")
    dp_count = lax.axis_size("dp")
    dp_index = lax.axis_index("dp")
    block_rows = query_weight.shape[1]

    query_full = stacked(gather_blocks(query_weight[0], "dp"))
    key_full = stacked(gather_blocks(key_weight[0], "dp"))
    value_full = stacked(gather_blocks(value_weight[0], "dp"))

    slot_rows = vision.shape[2]
    part_width = vision.shape[3]
    wanted = image_of[0, section]
    image_part = vision[0, 0]
    for steps in range(1, sections):
        moved = shifted(vision, "section", steps)[0, 0]
        image_part = jnp.where((section - steps) % sections == wanted, moved, image_part)
    image = lax.all_gather(image_part, "mp", axis=1, tiled=True)
    image_code = code_columns(image, dp_index, dp_count, block_rows)

    width_k = key_weight.shape[2]
    keys_raw = jnp.dot(image_code, key_full, preferred_element_type=jnp.float32).reshape(
        slot_rows, width_k // HD, HD
    )
    values_raw = jnp.dot(image_code, value_full, preferred_element_type=jnp.float32).reshape(
        slot_rows, width_k // HD, HD
    )
    usable = jnp.arange(slot_rows) < tile_counts[0, wanted] * TILE_ROWS

    text_rows = text_in.shape[2]
    width_q = query_weight.shape[2]
    chunks = 4 if text_rows % 32 == 0 else 1
    rows = text_rows // chunks
    contexts = []
    key_back = None
    value_back = None
    pieces = [
        shifted(text_in[:, :, chunk * rows : (chunk + 1) * rows, :], "section", 1)
        for chunk in range(chunks)
    ]
    first, image_code = lax.optimization_barrier((pieces[0], image_code))
    gathered = lax.all_gather(first, "mp", axis=3, tiled=True)
    for chunk in range(chunks):
        full_text = gathered[0, 0]
        if chunk + 1 < chunks:
            following, full_text = lax.optimization_barrier((pieces[chunk + 1], full_text))
            gathered = lax.all_gather(following, "mp", axis=3, tiled=True)
        normed = norm_rows(full_text, norm_gain[0]).astype(jnp.bfloat16)
        query_raw = jnp.dot(
            code_columns(normed, dp_index, dp_count, block_rows),
            query_full,
            preferred_element_type=jnp.float32,
        )
        queries = norm_rows(query_raw.reshape(rows, width_q // HD, HD), query_gain[0]).astype(
            jnp.bfloat16
        )
        present = chunk * rows + jnp.arange(rows) < lengths[0, 0]

        def forward(keys_in, values_in):
            return attend(queries, keys_in, values_in, key_gain[0], usable, present, cross_gate[0])

        context, pullback = jax.vjp(forward, keys_raw, values_raw)
        contexts.append(context.astype(jnp.bfloat16))
        key_part, value_part = pullback(
            context_grad[0, 0, chunk * rows : (chunk + 1) * rows].astype(jnp.float32)
        )
        key_back = key_part if key_back is None else key_back + key_part
        value_back = value_part if value_back is None else value_back + value_part
        if chunk + 1 < chunks:
            gathered, key_back, value_back = lax.optimization_barrier((gathered, key_back, value_back))
    gated_context = jnp.concatenate(contexts, axis=0).reshape(1, 1, text_rows, width_q)
    key_flat = key_back.reshape(slot_rows, width_k).astype(jnp.bfloat16)
    value_flat = value_back.reshape(slot_rows, width_k).astype(jnp.bfloat16)

    contract = (((1,), (1,)), ((), ()))
    partial_sum = lax.dot_general(key_flat, key_full, contract, preferred_element_type=jnp.float32)
    partial_sum = partial_sum + lax.dot_general(
        value_flat, value_full, contract, preferred_element_type=jnp.float32
    )
    partial_sum = code_columns(partial_sum.astype(jnp.bfloat16), dp_index, dp_count, block_rows)
    summed = lax.psum_scatter(partial_sum, "mp", scatter_dimension=1, tiled=True)

    routed = summed
    for steps in range(1, sections):
        moved = shifted(summed, "section", steps)
        source = (section - steps) % sections
        routed = jnp.where(image_of[0, source] == section, moved, routed)
    vision_grad = routed.reshape(1, 1, slot_rows, part_width)

    inner = (((0,), (0,)), ((), ()))
    key_grad = lax.dot_general(image_code, key_flat, inner, preferred_element_type=jnp.float32)
    value_grad = lax.dot_general(image_code, value_flat, inner, preferred_element_type=jnp.float32)
    both = jnp.concatenate([key_grad.astype(jnp.bfloat16), value_grad.astype(jnp.bfloat16)], axis=1)
    grad_blocks = {code: both[code * block_rows : (code + 1) * block_rows] for code in range(dp_count)}
    both_grads = scatter_blocks(grad_blocks, "dp").astype(jnp.bfloat16)
    key_weight_grad = both_grads[:, :width_k][None]
    value_weight_grad = both_grads[:, width_k:][None]
    return (gated_context, vision_grad, key_weight_grad, value_weight_grad)


def solution(mesh):
    return jax.shard_map(
        per_device,
        mesh=mesh,
        in_specs=(
            P("dp", "section", None, "mp"),
            P("dp", "section", None, "mp"),
            P("dp", None),
            P("dp", "section"),
            P("dp", None),
            P("section", None),
            P("section", "dp", "mp"),
            P("section", "dp", "mp"),
            P("section", "dp", "mp"),
            P("section", None),
            P("section", None),
            P("section"),
            P("dp", "section", None, "mp"),
        ),
        out_specs=(
            P("dp", "section", None, "mp"),
            P("dp", "section", None, "mp"),
            P("section", "dp", "mp"),
            P("section", "dp", "mp"),
        ),
        check_vma=False,
    )
```

```python
import jax
import jax.numpy as jnp
from jax import lax
from jax.sharding import PartitionSpec as P

HD = 128
TILE_ROWS = 64


def shifted(value, axis, steps):
    count = lax.axis_size(axis)
    pairs = [(source, (source + steps) % count) for source in range(count)]
    return lax.ppermute(value, axis, pairs)


def swapped(value, axis, mask):
    count = lax.axis_size(axis)
    pairs = [(source, source ^ mask) for source in range(count)]
    return lax.ppermute(value, axis, pairs)


def bit_order(count, high_first):
    bits = []
    step = 1
    while step < count:
        bits.append(step)
        step *= 2
    return bits[::-1] if high_first else bits


def gather_blocks(block, axis):
    count = lax.axis_size(axis)
    held = {0: block}
    for mask in bit_order(count, True):
        codes = sorted(held)
        arrived = swapped(jnp.stack([held[c] for c in codes]), axis, mask)
        for position, code in enumerate(codes):
            held[code ^ mask] = arrived[position]
    return held


def scatter_blocks(by_code, axis):
    count = lax.axis_size(axis)
    held = {code: value.astype(jnp.float32) for code, value in by_code.items()}
    for mask in bit_order(count, False):
        sent = sorted(c for c in held if c & mask)
        kept = [c ^ mask for c in sent]
        arrived = swapped(jnp.stack([held[c].astype(jnp.bfloat16) for c in sent]), axis, mask)
        held = {c: held[c] + arrived[position].astype(jnp.float32) for position, c in enumerate(kept)}
    return held[0]


def norm_rows(values, gain):
    values = values.astype(jnp.float32)
    scaled = values * lax.rsqrt(jnp.mean(values * values, axis=-1, keepdims=True) + 1e-05)
    return scaled * gain


def rounded(values):
    return lax.optimization_barrier(values.astype(jnp.bfloat16)).astype(jnp.float32)


def attend(queries, keys_raw, values_raw, key_norm, usable, present, gate_value):
    keys = rounded(norm_rows(keys_raw, key_norm))
    values = rounded(values_raw)
    text_rows, heads, depth = queries.shape
    groups = keys.shape[1]
    grouped = queries.astype(jnp.float32).reshape(text_rows, groups, heads // groups, depth)
    scores = jnp.einsum("tgjd,vgd->gjtv", grouped, keys) * depth ** (-0.5)
    scores = jnp.where(usable[None, None, None, :], scores, -1e30)
    highest = lax.stop_gradient(jnp.max(scores, axis=-1, keepdims=True))
    weights = jnp.exp(scores - highest)
    probs = rounded(weights / jnp.sum(weights, axis=-1, keepdims=True))
    context = jnp.einsum("gjtv,vgd->tgjd", probs, values).reshape(text_rows, heads * depth)
    return jnp.where(present[:, None], jnp.tanh(gate_value) * context, 0.0)


def columns_of(values, start, width):
    return lax.dynamic_slice_in_dim(values, start, width, axis=1)


def per_device(
    text_in,
    vision,
    tile_counts,
    lengths,
    image_of,
    norm_gain,
    query_weight,
    key_weight,
    value_weight,
    query_gain,
    key_gain,
    cross_gate,
    context_grad,
):
    sections = lax.axis_size("section")
    section = lax.axis_index("section")
    dp_index = lax.axis_index("dp")
    block_rows = query_weight.shape[1]

    query_blocks = gather_blocks(query_weight[0], "dp")
    key_blocks = gather_blocks(key_weight[0], "dp")
    value_blocks = gather_blocks(value_weight[0], "dp")

    slot_rows = vision.shape[2]
    part_width = vision.shape[3]
    wanted = image_of[0, section]
    image_part = vision[0, 0]
    for steps in range(1, sections):
        moved = shifted(vision, "section", steps)[0, 0]
        image_part = jnp.where((section - steps) % sections == wanted, moved, image_part)
    image = lax.all_gather(image_part, "mp", axis=1, tiled=True)

    width_k = key_weight.shape[2]
    keys_raw = None
    values_raw = None
    for code in key_blocks:
        piece = columns_of(image, (dp_index ^ code) * block_rows, block_rows)
        key_part = jnp.dot(piece, key_blocks[code], preferred_element_type=jnp.float32)
        value_part = jnp.dot(piece, value_blocks[code], preferred_element_type=jnp.float32)
        keys_raw = key_part if keys_raw is None else keys_raw + key_part
        values_raw = value_part if values_raw is None else values_raw + value_part
    keys_raw = keys_raw.reshape(slot_rows, width_k // HD, HD)
    values_raw = values_raw.reshape(slot_rows, width_k // HD, HD)
    usable = jnp.arange(slot_rows) < tile_counts[0, wanted] * TILE_ROWS

    arrived = shifted(text_in, "section", 1)
    text_rows = text_in.shape[2]
    width_q = query_weight.shape[2]
    chunks = 2 if text_rows % 16 == 0 else 1
    rows = text_rows // chunks
    contexts = []
    key_back = None
    value_back = None
    gathered = [
        lax.all_gather(arrived[:, :, chunk * rows : (chunk + 1) * rows], "mp", axis=3, tiled=True)
        for chunk in range(chunks)
    ]
    for chunk in range(chunks):
        lower = chunk * rows
        full_text = gathered[chunk][0, 0]
        normed = norm_rows(full_text, norm_gain[0]).astype(jnp.bfloat16)
        query_raw = None
        for code, block in query_blocks.items():
            part = jnp.dot(
                columns_of(normed, (dp_index ^ code) * block_rows, block_rows),
                block,
                preferred_element_type=jnp.float32,
            )
            query_raw = part if query_raw is None else query_raw + part
        queries = norm_rows(query_raw.reshape(rows, width_q // HD, HD), query_gain[0]).astype(
            jnp.bfloat16
        )
        present = lower + jnp.arange(rows) < lengths[0, 0]

        def forward(keys_in, values_in):
            return attend(queries, keys_in, values_in, key_gain[0], usable, present, cross_gate[0])

        context, pullback = jax.vjp(forward, keys_raw, values_raw)
        contexts.append(context.astype(jnp.bfloat16))
        key_part, value_part = pullback(context_grad[0, 0, lower : lower + rows].astype(jnp.float32))
        key_back = key_part if key_back is None else key_back + key_part
        value_back = value_part if value_back is None else value_back + value_part
        if chunk + 1 < chunks:
            gathered[chunk + 1], key_back, value_back = lax.optimization_barrier(
                (gathered[chunk + 1], key_back, value_back)
            )
    gated_context = jnp.concatenate(contexts, axis=0).reshape(1, 1, text_rows, width_q)
    key_flat = key_back.reshape(slot_rows, width_k).astype(jnp.bfloat16)
    value_flat = value_back.reshape(slot_rows, width_k).astype(jnp.bfloat16)

    contract = (((1,), (1,)), ((), ()))
    partial_sum = jnp.zeros((slot_rows, image.shape[1]), jnp.bfloat16)
    for code in key_blocks:
        term = lax.dot_general(key_flat, key_blocks[code], contract, preferred_element_type=jnp.float32)
        term = term + lax.dot_general(
            value_flat, value_blocks[code], contract, preferred_element_type=jnp.float32
        )
        partial_sum = lax.dynamic_update_slice_in_dim(
            partial_sum, term.astype(jnp.bfloat16), (dp_index ^ code) * block_rows, axis=1
        )
    summed = lax.psum_scatter(partial_sum, "mp", scatter_dimension=1, tiled=True)

    routed = summed
    for steps in range(1, sections):
        moved = shifted(summed, "section", steps)
        source = (section - steps) % sections
        routed = jnp.where(image_of[0, source] == section, moved, routed)
    vision_grad = routed.reshape(1, 1, slot_rows, part_width)

    inner = (((0,), (0,)), ((), ()))
    grad_blocks = {}
    for code in key_blocks:
        piece = columns_of(image, (dp_index ^ code) * block_rows, block_rows)
        key_part = lax.dot_general(piece, key_flat, inner, preferred_element_type=jnp.float32)
        value_part = lax.dot_general(piece, value_flat, inner, preferred_element_type=jnp.float32)
        grad_blocks[code] = jnp.concatenate(
            [key_part.astype(jnp.bfloat16), value_part.astype(jnp.bfloat16)], axis=1
        )
    both_grads = scatter_blocks(grad_blocks, "dp").astype(jnp.bfloat16)
    key_weight_grad = both_grads[:, :width_k][None]
    value_weight_grad = both_grads[:, width_k:][None]
    return (gated_context, vision_grad, key_weight_grad, value_weight_grad)


def solution(mesh):
    return jax.shard_map(
        per_device,
        mesh=mesh,
        in_specs=(
            P("dp", "section", None, "mp"),
            P("dp", "section", None, "mp"),
            P("dp", None),
            P("dp", "section"),
            P("dp", None),
            P("section", None),
            P("section", "dp", "mp"),
            P("section", "dp", "mp"),
            P("section", "dp", "mp"),
            P("section", None),
            P("section", None),
            P("section"),
            P("dp", "section", None, "mp"),
        ),
        out_specs=(
            P("dp", "section", None, "mp"),
            P("dp", "section", None, "mp"),
            P("section", "dp", "mp"),
            P("section", "dp", "mp"),
        ),
        check_vma=False,
    )
```

```python
import jax
import jax.numpy as jnp
from jax import lax
from jax.sharding import PartitionSpec as P

HD = 128
TILE_ROWS = 64


def shifted(value, axis, steps):
    count = lax.axis_size(axis)
    pairs = [(source, (source + steps) % count) for source in range(count)]
    return lax.ppermute(value, axis, pairs)


def swapped(value, axis, mask):
    count = lax.axis_size(axis)
    pairs = [(source, source ^ mask) for source in range(count)]
    return lax.ppermute(value, axis, pairs)


def bit_order(count, high_first):
    bits = []
    step = 1
    while step < count:
        bits.append(step)
        step *= 2
    return bits[::-1] if high_first else bits


def gather_blocks(block, axis):
    count = lax.axis_size(axis)
    held = {0: block}
    for mask in bit_order(count, True):
        codes = sorted(held)
        arrived = swapped(jnp.stack([held[c] for c in codes]), axis, mask)
        for position, code in enumerate(codes):
            held[code ^ mask] = arrived[position]
    return held


def scatter_blocks(by_code, axis):
    count = lax.axis_size(axis)
    held = {code: value.astype(jnp.float32) for code, value in by_code.items()}
    for mask in bit_order(count, False):
        sent = sorted(c for c in held if c & mask)
        kept = [c ^ mask for c in sent]
        arrived = swapped(jnp.stack([held[c].astype(jnp.bfloat16) for c in sent]), axis, mask)
        held = {c: held[c] + arrived[position].astype(jnp.float32) for position, c in enumerate(kept)}
    return held[0]


def norm_rows(values, gain):
    values = values.astype(jnp.float32)
    scaled = values * lax.rsqrt(jnp.mean(values * values, axis=-1, keepdims=True) + 1e-05)
    return scaled * gain


def rounded(values):
    return lax.optimization_barrier(values.astype(jnp.bfloat16)).astype(jnp.float32)


def attend(queries, keys_raw, values_raw, key_norm, usable, present, gate_value):
    keys = rounded(norm_rows(keys_raw, key_norm))
    values = rounded(values_raw)
    text_rows, heads, depth = queries.shape
    groups = keys.shape[1]
    grouped = queries.astype(jnp.float32).reshape(text_rows, groups, heads // groups, depth)
    scores = jnp.einsum("tgjd,vgd->gjtv", grouped, keys) * depth ** (-0.5)
    scores = jnp.where(usable[None, None, None, :], scores, -1e30)
    highest = lax.stop_gradient(jnp.max(scores, axis=-1, keepdims=True))
    weights = jnp.exp(scores - highest)
    probs = rounded(weights / jnp.sum(weights, axis=-1, keepdims=True))
    context = jnp.einsum("gjtv,vgd->tgjd", probs, values).reshape(text_rows, heads * depth)
    return jnp.where(present[:, None], jnp.tanh(gate_value) * context, 0.0)


def columns_of(values, start, width):
    return lax.dynamic_slice_in_dim(values, start, width, axis=1)


def per_device(
    text_in,
    vision,
    tile_counts,
    lengths,
    image_of,
    norm_gain,
    query_weight,
    key_weight,
    value_weight,
    query_gain,
    key_gain,
    cross_gate,
    context_grad,
):
    sections = lax.axis_size("section")
    section = lax.axis_index("section")
    dp_index = lax.axis_index("dp")
    block_rows = query_weight.shape[1]

    query_blocks = gather_blocks(query_weight[0], "dp")
    key_blocks = gather_blocks(key_weight[0], "dp")
    value_blocks = gather_blocks(value_weight[0], "dp")

    slot_rows = vision.shape[2]
    part_width = vision.shape[3]
    wanted = image_of[0, section]
    owned = lax.all_gather(vision[0, 0], "mp", axis=1, tiled=True)
    image = owned
    for steps in range(1, sections):
        moved = shifted(owned, "section", steps)
        image = jnp.where((section - steps) % sections == wanted, moved, image)

    width_k = key_weight.shape[2]
    keys_raw = None
    values_raw = None
    for code in key_blocks:
        piece = columns_of(image, (dp_index ^ code) * block_rows, block_rows)
        key_part = jnp.dot(piece, key_blocks[code], preferred_element_type=jnp.float32)
        value_part = jnp.dot(piece, value_blocks[code], preferred_element_type=jnp.float32)
        keys_raw = key_part if keys_raw is None else keys_raw + key_part
        values_raw = value_part if values_raw is None else values_raw + value_part
    keys_raw = keys_raw.reshape(slot_rows, width_k // HD, HD)
    values_raw = values_raw.reshape(slot_rows, width_k // HD, HD)
    usable = jnp.arange(slot_rows) < tile_counts[0, wanted] * TILE_ROWS

    arrived = shifted(text_in, "section", 1)
    text_rows = text_in.shape[2]
    width_q = query_weight.shape[2]
    chunks = 2 if text_rows % 16 == 0 else 1
    rows = text_rows // chunks
    contexts = []
    key_back = None
    value_back = None
    gathered = [
        lax.all_gather(arrived[:, :, chunk * rows : (chunk + 1) * rows], "mp", axis=3, tiled=True)
        for chunk in range(chunks)
    ]
    for chunk in range(chunks):
        lower = chunk * rows
        full_text = gathered[chunk][0, 0]
        normed = norm_rows(full_text, norm_gain[0]).astype(jnp.bfloat16)
        query_raw = None
        for code, block in query_blocks.items():
            part = jnp.dot(
                columns_of(normed, (dp_index ^ code) * block_rows, block_rows),
                block,
                preferred_element_type=jnp.float32,
            )
            query_raw = part if query_raw is None else query_raw + part
        queries = norm_rows(query_raw.reshape(rows, width_q // HD, HD), query_gain[0]).astype(
            jnp.bfloat16
        )
        present = lower + jnp.arange(rows) < lengths[0, 0]

        def forward(keys_in, values_in):
            return attend(queries, keys_in, values_in, key_gain[0], usable, present, cross_gate[0])

        context, pullback = jax.vjp(forward, keys_raw, values_raw)
        contexts.append(context.astype(jnp.bfloat16))
        key_part, value_part = pullback(context_grad[0, 0, lower : lower + rows].astype(jnp.float32))
        key_back = key_part if key_back is None else key_back + key_part
        value_back = value_part if value_back is None else value_back + value_part
        if chunk + 1 < chunks:
            gathered[chunk + 1], key_back, value_back = lax.optimization_barrier(
                (gathered[chunk + 1], key_back, value_back)
            )
    gated_context = jnp.concatenate(contexts, axis=0).reshape(1, 1, text_rows, width_q)
    key_flat = key_back.reshape(slot_rows, width_k).astype(jnp.bfloat16)
    value_flat = value_back.reshape(slot_rows, width_k).astype(jnp.bfloat16)

    contract = (((1,), (1,)), ((), ()))
    partial_sum = jnp.zeros((slot_rows, image.shape[1]), jnp.bfloat16)
    for code in key_blocks:
        term = lax.dot_general(key_flat, key_blocks[code], contract, preferred_element_type=jnp.float32)
        term = term + lax.dot_general(
            value_flat, value_blocks[code], contract, preferred_element_type=jnp.float32
        )
        partial_sum = lax.dynamic_update_slice_in_dim(
            partial_sum, term.astype(jnp.bfloat16), (dp_index ^ code) * block_rows, axis=1
        )
    summed = lax.psum_scatter(partial_sum, "mp", scatter_dimension=1, tiled=True)

    routed = summed
    for steps in range(1, sections):
        moved = shifted(summed, "section", steps)
        source = (section - steps) % sections
        routed = jnp.where(image_of[0, source] == section, moved, routed)
    vision_grad = routed.reshape(1, 1, slot_rows, part_width)

    inner = (((0,), (0,)), ((), ()))
    grad_blocks = {}
    for code in key_blocks:
        piece = columns_of(image, (dp_index ^ code) * block_rows, block_rows)
        key_part = lax.dot_general(piece, key_flat, inner, preferred_element_type=jnp.float32)
        value_part = lax.dot_general(piece, value_flat, inner, preferred_element_type=jnp.float32)
        grad_blocks[code] = jnp.concatenate(
            [key_part.astype(jnp.bfloat16), value_part.astype(jnp.bfloat16)], axis=1
        )
    both_grads = scatter_blocks(grad_blocks, "dp").astype(jnp.bfloat16)
    key_weight_grad = both_grads[:, :width_k][None]
    value_weight_grad = both_grads[:, width_k:][None]
    return (gated_context, vision_grad, key_weight_grad, value_weight_grad)


def solution(mesh):
    return jax.shard_map(
        per_device,
        mesh=mesh,
        in_specs=(
            P("dp", "section", None, "mp"),
            P("dp", "section", None, "mp"),
            P("dp", None),
            P("dp", "section"),
            P("dp", None),
            P("section", None),
            P("section", "dp", "mp"),
            P("section", "dp", "mp"),
            P("section", "dp", "mp"),
            P("section", None),
            P("section", None),
            P("section"),
            P("dp", "section", None, "mp"),
        ),
        out_specs=(
            P("dp", "section", None, "mp"),
            P("dp", "section", None, "mp"),
            P("section", "dp", "mp"),
            P("section", "dp", "mp"),
        ),
        check_vma=False,
    )
```

```python
import jax
import jax.numpy as jnp
from jax import lax
from jax.sharding import PartitionSpec as P

HD = 128
TILE_ROWS = 64


def shifted(value, axis, steps):
    count = lax.axis_size(axis)
    pairs = [(source, (source + steps) % count) for source in range(count)]
    return lax.ppermute(value, axis, pairs)


def swapped(value, axis, mask):
    count = lax.axis_size(axis)
    pairs = [(source, source ^ mask) for source in range(count)]
    return lax.ppermute(value, axis, pairs)


def bit_order(count, high_first):
    bits = []
    step = 1
    while step < count:
        bits.append(step)
        step *= 2
    return bits[::-1] if high_first else bits


def gather_blocks(block, axis):
    count = lax.axis_size(axis)
    held = {0: block}
    for mask in bit_order(count, True):
        codes = sorted(held)
        arrived = swapped(jnp.stack([held[c] for c in codes]), axis, mask)
        for position, code in enumerate(codes):
            held[code ^ mask] = arrived[position]
    return held


def gather_direct(block, axis):
    count = lax.axis_size(axis)
    held = {0: block}
    for mask in range(1, count):
        held[mask] = swapped(block, axis, mask)
    return held


def scatter_blocks(by_code, axis):
    count = lax.axis_size(axis)
    held = {code: value.astype(jnp.float32) for code, value in by_code.items()}
    for mask in bit_order(count, False):
        sent = sorted(c for c in held if c & mask)
        kept = [c ^ mask for c in sent]
        arrived = swapped(jnp.stack([held[c].astype(jnp.bfloat16) for c in sent]), axis, mask)
        held = {c: held[c] + arrived[position].astype(jnp.float32) for position, c in enumerate(kept)}
    return held[0]


def norm_rows(values, gain):
    values = values.astype(jnp.float32)
    scaled = values * lax.rsqrt(jnp.mean(values * values, axis=-1, keepdims=True) + 1e-05)
    return scaled * gain


def rounded(values):
    return lax.optimization_barrier(values.astype(jnp.bfloat16)).astype(jnp.float32)


def attend(queries, keys_raw, values_raw, key_norm, usable, present, gate_value):
    keys = rounded(norm_rows(keys_raw, key_norm))
    values = rounded(values_raw)
    text_rows, heads, depth = queries.shape
    groups = keys.shape[1]
    grouped = queries.astype(jnp.float32).reshape(text_rows, groups, heads // groups, depth)
    scores = jnp.einsum("tgjd,vgd->gjtv", grouped, keys) * depth ** (-0.5)
    scores = jnp.where(usable[None, None, None, :], scores, -1e30)
    highest = lax.stop_gradient(jnp.max(scores, axis=-1, keepdims=True))
    weights = jnp.exp(scores - highest)
    probs = rounded(weights / jnp.sum(weights, axis=-1, keepdims=True))
    context = jnp.einsum("gjtv,vgd->tgjd", probs, values).reshape(text_rows, heads * depth)
    return jnp.where(present[:, None], jnp.tanh(gate_value) * context, 0.0)


def columns_of(values, start, width):
    return lax.dynamic_slice_in_dim(values, start, width, axis=1)


def per_device(
    text_in,
    vision,
    tile_counts,
    lengths,
    image_of,
    norm_gain,
    query_weight,
    key_weight,
    value_weight,
    query_gain,
    key_gain,
    cross_gate,
    context_grad,
):
    sections = lax.axis_size("section")
    section = lax.axis_index("section")
    dp_index = lax.axis_index("dp")
    block_rows = query_weight.shape[1]

    key_blocks = gather_direct(key_weight[0], "dp")
    value_blocks = gather_direct(value_weight[0], "dp")

    slot_rows = vision.shape[2]
    part_width = vision.shape[3]
    wanted = image_of[0, section]
    owned = lax.all_gather(vision[0, 0], "mp", axis=1, tiled=True)
    image = owned
    for steps in range(1, sections):
        moved = shifted(owned, "section", steps)
        image = jnp.where((section - steps) % sections == wanted, moved, image)

    width_k = key_weight.shape[2]
    keys_raw = None
    values_raw = None
    for code in key_blocks:
        piece = columns_of(image, (dp_index ^ code) * block_rows, block_rows)
        key_part = jnp.dot(piece, key_blocks[code], preferred_element_type=jnp.float32)
        value_part = jnp.dot(piece, value_blocks[code], preferred_element_type=jnp.float32)
        keys_raw = key_part if keys_raw is None else keys_raw + key_part
        values_raw = value_part if values_raw is None else values_raw + value_part
    keys_raw = keys_raw.reshape(slot_rows, width_k // HD, HD)
    values_raw = values_raw.reshape(slot_rows, width_k // HD, HD)
    usable = jnp.arange(slot_rows) < tile_counts[0, wanted] * TILE_ROWS

    arrived = shifted(text_in, "section", 1)
    query_blocks = gather_blocks(query_weight[0], "dp")
    text_rows = text_in.shape[2]
    width_q = query_weight.shape[2]
    chunks = 2 if text_rows % 16 == 0 else 1
    rows = text_rows // chunks
    contexts = []
    key_back = None
    value_back = None
    gathered = [
        lax.all_gather(arrived[:, :, chunk * rows : (chunk + 1) * rows], "mp", axis=3, tiled=True)
        for chunk in range(chunks)
    ]
    for chunk in range(chunks):
        lower = chunk * rows
        full_text = gathered[chunk][0, 0]
        normed = norm_rows(full_text, norm_gain[0]).astype(jnp.bfloat16)
        query_raw = None
        for code, block in query_blocks.items():
            part = jnp.dot(
                columns_of(normed, (dp_index ^ code) * block_rows, block_rows),
                block,
                preferred_element_type=jnp.float32,
            )
            query_raw = part if query_raw is None else query_raw + part
        queries = norm_rows(query_raw.reshape(rows, width_q // HD, HD), query_gain[0]).astype(
            jnp.bfloat16
        )
        present = lower + jnp.arange(rows) < lengths[0, 0]

        def forward(keys_in, values_in):
            return attend(queries, keys_in, values_in, key_gain[0], usable, present, cross_gate[0])

        context, pullback = jax.vjp(forward, keys_raw, values_raw)
        contexts.append(context.astype(jnp.bfloat16))
        key_part, value_part = pullback(context_grad[0, 0, lower : lower + rows].astype(jnp.float32))
        key_back = key_part if key_back is None else key_back + key_part
        value_back = value_part if value_back is None else value_back + value_part
        if chunk + 1 < chunks:
            gathered[chunk + 1], key_back, value_back = lax.optimization_barrier(
                (gathered[chunk + 1], key_back, value_back)
            )
    gated_context = jnp.concatenate(contexts, axis=0).reshape(1, 1, text_rows, width_q)
    key_flat = key_back.reshape(slot_rows, width_k).astype(jnp.bfloat16)
    value_flat = value_back.reshape(slot_rows, width_k).astype(jnp.bfloat16)

    contract = (((1,), (1,)), ((), ()))
    partial_sum = jnp.zeros((slot_rows, image.shape[1]), jnp.bfloat16)
    for code in key_blocks:
        term = lax.dot_general(key_flat, key_blocks[code], contract, preferred_element_type=jnp.float32)
        term = term + lax.dot_general(
            value_flat, value_blocks[code], contract, preferred_element_type=jnp.float32
        )
        partial_sum = lax.dynamic_update_slice_in_dim(
            partial_sum, term.astype(jnp.bfloat16), (dp_index ^ code) * block_rows, axis=1
        )
    summed = lax.psum_scatter(partial_sum, "mp", scatter_dimension=1, tiled=True)

    routed = summed
    for steps in range(1, sections):
        moved = shifted(summed, "section", steps)
        source = (section - steps) % sections
        routed = jnp.where(image_of[0, source] == section, moved, routed)
    vision_grad = routed.reshape(1, 1, slot_rows, part_width)

    inner = (((0,), (0,)), ((), ()))
    grad_blocks = {}
    for code in key_blocks:
        piece = columns_of(image, (dp_index ^ code) * block_rows, block_rows)
        key_part = lax.dot_general(piece, key_flat, inner, preferred_element_type=jnp.float32)
        value_part = lax.dot_general(piece, value_flat, inner, preferred_element_type=jnp.float32)
        grad_blocks[code] = jnp.concatenate(
            [key_part.astype(jnp.bfloat16), value_part.astype(jnp.bfloat16)], axis=1
        )
    both_grads = scatter_blocks(grad_blocks, "dp").astype(jnp.bfloat16)
    key_weight_grad = both_grads[:, :width_k][None]
    value_weight_grad = both_grads[:, width_k:][None]
    return (gated_context, vision_grad, key_weight_grad, value_weight_grad)


def solution(mesh):
    return jax.shard_map(
        per_device,
        mesh=mesh,
        in_specs=(
            P("dp", "section", None, "mp"),
            P("dp", "section", None, "mp"),
            P("dp", None),
            P("dp", "section"),
            P("dp", None),
            P("section", None),
            P("section", "dp", "mp"),
            P("section", "dp", "mp"),
            P("section", "dp", "mp"),
            P("section", None),
            P("section", None),
            P("section"),
            P("dp", "section", None, "mp"),
        ),
        out_specs=(
            P("dp", "section", None, "mp"),
            P("dp", "section", None, "mp"),
            P("section", "dp", "mp"),
            P("section", "dp", "mp"),
        ),
        check_vma=False,
    )
```

```python
import jax
import jax.numpy as jnp
from jax import lax
from jax.sharding import PartitionSpec as P

HD = 128
TILE_ROWS = 64


def shifted(value, axis, steps):
    count = lax.axis_size(axis)
    pairs = [(source, (source + steps) % count) for source in range(count)]
    return lax.ppermute(value, axis, pairs)


def swapped(value, axis, mask):
    count = lax.axis_size(axis)
    pairs = [(source, source ^ mask) for source in range(count)]
    return lax.ppermute(value, axis, pairs)


def bit_order(count, high_first):
    bits = []
    step = 1
    while step < count:
        bits.append(step)
        step *= 2
    return bits[::-1] if high_first else bits


def gather_blocks(block, axis):
    count = lax.axis_size(axis)
    held = {0: block}
    for mask in bit_order(count, True):
        codes = sorted(held)
        arrived = swapped(jnp.stack([held[c] for c in codes]), axis, mask)
        for position, code in enumerate(codes):
            held[code ^ mask] = arrived[position]
    return held


def gather_direct(block, axis):
    count = lax.axis_size(axis)
    held = {0: block}
    for mask in range(1, count):
        held[mask] = swapped(block, axis, mask)
    return held


def scatter_blocks(by_code, axis):
    count = lax.axis_size(axis)
    held = {code: value.astype(jnp.float32) for code, value in by_code.items()}
    for mask in bit_order(count, False):
        sent = sorted(c for c in held if c & mask)
        kept = [c ^ mask for c in sent]
        arrived = swapped(jnp.stack([held[c].astype(jnp.bfloat16) for c in sent]), axis, mask)
        held = {c: held[c] + arrived[position].astype(jnp.float32) for position, c in enumerate(kept)}
    return held[0]


def norm_rows(values, gain):
    values = values.astype(jnp.float32)
    scaled = values * lax.rsqrt(jnp.mean(values * values, axis=-1, keepdims=True) + 1e-05)
    return scaled * gain


def rounded(values):
    return lax.optimization_barrier(values.astype(jnp.bfloat16)).astype(jnp.float32)


def attend(queries, keys_raw, values_raw, key_norm, usable, present, gate_value):
    keys = rounded(norm_rows(keys_raw, key_norm))
    values = rounded(values_raw)
    text_rows, heads, depth = queries.shape
    groups = keys.shape[1]
    grouped = queries.astype(jnp.float32).reshape(text_rows, groups, heads // groups, depth)
    scores = jnp.einsum("tgjd,vgd->gjtv", grouped, keys) * depth ** (-0.5)
    scores = jnp.where(usable[None, None, None, :], scores, -1e30)
    highest = lax.stop_gradient(jnp.max(scores, axis=-1, keepdims=True))
    weights = jnp.exp(scores - highest)
    probs = rounded(weights / jnp.sum(weights, axis=-1, keepdims=True))
    context = jnp.einsum("gjtv,vgd->tgjd", probs, values).reshape(text_rows, heads * depth)
    return jnp.where(present[:, None], jnp.tanh(gate_value) * context, 0.0)


def columns_of(values, start, width):
    return lax.dynamic_slice_in_dim(values, start, width, axis=1)


def per_device(
    text_in,
    vision,
    tile_counts,
    lengths,
    image_of,
    norm_gain,
    query_weight,
    key_weight,
    value_weight,
    query_gain,
    key_gain,
    cross_gate,
    context_grad,
):
    sections = lax.axis_size("section")
    section = lax.axis_index("section")
    dp_index = lax.axis_index("dp")
    block_rows = query_weight.shape[1]

    width_k = key_weight.shape[2]
    pair_blocks = gather_blocks(jnp.concatenate([key_weight[0], value_weight[0]], axis=1), "dp")

    slot_rows = vision.shape[2]
    part_width = vision.shape[3]
    wanted = image_of[0, section]
    owned = lax.all_gather(vision[0, 0], "mp", axis=1, tiled=True)
    image = owned
    for steps in range(1, sections):
        moved = shifted(owned, "section", steps)
        image = jnp.where((section - steps) % sections == wanted, moved, image)

    pair_raw = None
    for code in pair_blocks:
        piece = columns_of(image, (dp_index ^ code) * block_rows, block_rows)
        part = jnp.dot(piece, pair_blocks[code], preferred_element_type=jnp.float32)
        pair_raw = part if pair_raw is None else pair_raw + part
    keys_raw = pair_raw[:, :width_k].reshape(slot_rows, width_k // HD, HD)
    values_raw = pair_raw[:, width_k:].reshape(slot_rows, width_k // HD, HD)
    usable = jnp.arange(slot_rows) < tile_counts[0, wanted] * TILE_ROWS

    arrived = shifted(text_in, "section", 1)
    query_local, pair_blocks = lax.optimization_barrier((query_weight[0], pair_blocks))
    query_blocks = gather_blocks(query_local, "dp")
    text_rows = text_in.shape[2]
    width_q = query_weight.shape[2]
    chunks = 2 if text_rows % 16 == 0 else 1
    rows = text_rows // chunks
    contexts = []
    key_back = None
    value_back = None
    gathered = [
        lax.all_gather(arrived[:, :, chunk * rows : (chunk + 1) * rows], "mp", axis=3, tiled=True)
        for chunk in range(chunks)
    ]
    for chunk in range(chunks):
        lower = chunk * rows
        full_text = gathered[chunk][0, 0]
        normed = norm_rows(full_text, norm_gain[0]).astype(jnp.bfloat16)
        query_raw = None
        for code, block in query_blocks.items():
            part = jnp.dot(
                columns_of(normed, (dp_index ^ code) * block_rows, block_rows),
                block,
                preferred_element_type=jnp.float32,
            )
            query_raw = part if query_raw is None else query_raw + part
        queries = norm_rows(query_raw.reshape(rows, width_q // HD, HD), query_gain[0]).astype(
            jnp.bfloat16
        )
        present = lower + jnp.arange(rows) < lengths[0, 0]

        def forward(keys_in, values_in):
            return attend(queries, keys_in, values_in, key_gain[0], usable, present, cross_gate[0])

        context, pullback = jax.vjp(forward, keys_raw, values_raw)
        contexts.append(context.astype(jnp.bfloat16))
        key_part, value_part = pullback(context_grad[0, 0, lower : lower + rows].astype(jnp.float32))
        key_back = key_part if key_back is None else key_back + key_part
        value_back = value_part if value_back is None else value_back + value_part
        if chunk + 1 < chunks:
            gathered[chunk + 1], key_back, value_back = lax.optimization_barrier(
                (gathered[chunk + 1], key_back, value_back)
            )
    gated_context = jnp.concatenate(contexts, axis=0).reshape(1, 1, text_rows, width_q)
    key_flat = key_back.reshape(slot_rows, width_k).astype(jnp.bfloat16)
    value_flat = value_back.reshape(slot_rows, width_k).astype(jnp.bfloat16)

    contract = (((1,), (1,)), ((), ()))
    partial_sum = jnp.zeros((slot_rows, image.shape[1]), jnp.bfloat16)
    pair_flat = jnp.concatenate([key_flat, value_flat], axis=1)
    for code in pair_blocks:
        term = lax.dot_general(pair_flat, pair_blocks[code], contract, preferred_element_type=jnp.float32)
        partial_sum = lax.dynamic_update_slice_in_dim(
            partial_sum, term.astype(jnp.bfloat16), (dp_index ^ code) * block_rows, axis=1
        )
    summed = lax.psum_scatter(partial_sum, "mp", scatter_dimension=1, tiled=True)

    routed = summed
    for steps in range(1, sections):
        moved = shifted(summed, "section", steps)
        source = (section - steps) % sections
        routed = jnp.where(image_of[0, source] == section, moved, routed)
    vision_grad = routed.reshape(1, 1, slot_rows, part_width)

    inner = (((0,), (0,)), ((), ()))
    grad_blocks = {}
    for code in pair_blocks:
        piece = columns_of(image, (dp_index ^ code) * block_rows, block_rows)
        key_part = lax.dot_general(piece, key_flat, inner, preferred_element_type=jnp.float32)
        value_part = lax.dot_general(piece, value_flat, inner, preferred_element_type=jnp.float32)
        grad_blocks[code] = jnp.concatenate(
            [key_part.astype(jnp.bfloat16), value_part.astype(jnp.bfloat16)], axis=1
        )
    both_grads = scatter_blocks(grad_blocks, "dp").astype(jnp.bfloat16)
    key_weight_grad = both_grads[:, :width_k][None]
    value_weight_grad = both_grads[:, width_k:][None]
    return (gated_context, vision_grad, key_weight_grad, value_weight_grad)


def solution(mesh):
    return jax.shard_map(
        per_device,
        mesh=mesh,
        in_specs=(
            P("dp", "section", None, "mp"),
            P("dp", "section", None, "mp"),
            P("dp", None),
            P("dp", "section"),
            P("dp", None),
            P("section", None),
            P("section", "dp", "mp"),
            P("section", "dp", "mp"),
            P("section", "dp", "mp"),
            P("section", None),
            P("section", None),
            P("section"),
            P("dp", "section", None, "mp"),
        ),
        out_specs=(
            P("dp", "section", None, "mp"),
            P("dp", "section", None, "mp"),
            P("section", "dp", "mp"),
            P("section", "dp", "mp"),
        ),
        check_vma=False,
    )
```

```python
import jax
import jax.numpy as jnp
from jax import lax
from jax.sharding import PartitionSpec as P

HD = 128
TILE_ROWS = 64


def shifted(value, axis, steps):
    count = lax.axis_size(axis)
    pairs = [(source, (source + steps) % count) for source in range(count)]
    return lax.ppermute(value, axis, pairs)


def swapped(value, axis, mask):
    count = lax.axis_size(axis)
    pairs = [(source, source ^ mask) for source in range(count)]
    return lax.ppermute(value, axis, pairs)


def bit_order(count, high_first):
    bits = []
    step = 1
    while step < count:
        bits.append(step)
        step *= 2
    return bits[::-1] if high_first else bits


def gather_blocks(block, axis):
    count = lax.axis_size(axis)
    held = {0: block}
    for mask in bit_order(count, True):
        codes = sorted(held)
        arrived = swapped(jnp.stack([held[c] for c in codes]), axis, mask)
        for position, code in enumerate(codes):
            held[code ^ mask] = arrived[position]
    return held


def scatter_blocks(by_code, axis):
    count = lax.axis_size(axis)
    held = {code: value.astype(jnp.float32) for code, value in by_code.items()}
    for mask in bit_order(count, False):
        sent = sorted(c for c in held if c & mask)
        kept = [c ^ mask for c in sent]
        arrived = swapped(jnp.stack([held[c].astype(jnp.bfloat16) for c in sent]), axis, mask)
        held = {c: held[c] + arrived[position].astype(jnp.float32) for position, c in enumerate(kept)}
    return held[0]


def norm_rows(values, gain):
    values = values.astype(jnp.float32)
    scaled = values * lax.rsqrt(jnp.mean(values * values, axis=-1, keepdims=True) + 1e-05)
    return scaled * gain


def rounded(values):
    return lax.optimization_barrier(values.astype(jnp.bfloat16)).astype(jnp.float32)


def attend(queries, keys_raw, values_raw, key_norm, usable, present, gate_value):
    keys = rounded(norm_rows(keys_raw, key_norm))
    values = rounded(values_raw)
    text_rows, heads, depth = queries.shape
    groups = keys.shape[1]
    grouped = queries.astype(jnp.float32).reshape(text_rows, groups, heads // groups, depth)
    scores = jnp.einsum("tgjd,vgd->gjtv", grouped, keys) * depth ** (-0.5)
    scores = jnp.where(usable[None, None, None, :], scores, -1e30)
    highest = lax.stop_gradient(jnp.max(scores, axis=-1, keepdims=True))
    weights = jnp.exp(scores - highest)
    probs = rounded(weights / jnp.sum(weights, axis=-1, keepdims=True))
    context = jnp.einsum("gjtv,vgd->tgjd", probs, values).reshape(text_rows, heads * depth)
    return jnp.where(present[:, None], jnp.tanh(gate_value) * context, 0.0)


def columns_of(values, start, width):
    return lax.dynamic_slice_in_dim(values, start, width, axis=1)


def per_device(
    text_in,
    vision,
    tile_counts,
    lengths,
    image_of,
    norm_gain,
    query_weight,
    key_weight,
    value_weight,
    query_gain,
    key_gain,
    cross_gate,
    context_grad,
):
    sections = lax.axis_size("section")
    section = lax.axis_index("section")
    dp_index = lax.axis_index("dp")
    block_rows = query_weight.shape[1]

    query_blocks = gather_blocks(query_weight[0], "dp")
    key_blocks = gather_blocks(key_weight[0], "dp")
    value_blocks = gather_blocks(value_weight[0], "dp")

    slot_rows = vision.shape[2]
    part_width = vision.shape[3]
    wanted = image_of[0, section]
    image_part = vision[0, 0]
    for steps in range(1, sections):
        moved = shifted(vision, "section", steps)[0, 0]
        image_part = jnp.where((section - steps) % sections == wanted, moved, image_part)
    image = lax.all_gather(image_part, "mp", axis=1, tiled=True)

    width_k = key_weight.shape[2]
    keys_raw = None
    values_raw = None
    for code in key_blocks:
        piece = columns_of(image, (dp_index ^ code) * block_rows, block_rows)
        key_part = jnp.dot(piece, key_blocks[code], preferred_element_type=jnp.float32)
        value_part = jnp.dot(piece, value_blocks[code], preferred_element_type=jnp.float32)
        keys_raw = key_part if keys_raw is None else keys_raw + key_part
        values_raw = value_part if values_raw is None else values_raw + value_part
    keys_raw = keys_raw.reshape(slot_rows, width_k // HD, HD)
    values_raw = values_raw.reshape(slot_rows, width_k // HD, HD)
    usable = jnp.arange(slot_rows) < tile_counts[0, wanted] * TILE_ROWS

    arrived = shifted(text_in, "section", 1)
    text_rows = text_in.shape[2]
    width_q = query_weight.shape[2]
    if text_rows % 64 == 0:
        bounds = [0, text_rows // 2, text_rows * 3 // 4, text_rows]
    else:
        bounds = [0, text_rows]
    chunks = len(bounds) - 1
    contexts = []
    key_back = None
    value_back = None
    gathered = [
        lax.all_gather(arrived[:, :, bounds[chunk] : bounds[chunk + 1]], "mp", axis=3, tiled=True)
        for chunk in range(chunks)
    ]
    for chunk in range(chunks):
        lower = bounds[chunk]
        rows = bounds[chunk + 1] - lower
        full_text = gathered[chunk][0, 0]
        normed = norm_rows(full_text, norm_gain[0]).astype(jnp.bfloat16)
        query_raw = None
        for code, block in query_blocks.items():
            part = jnp.dot(
                columns_of(normed, (dp_index ^ code) * block_rows, block_rows),
                block,
                preferred_element_type=jnp.float32,
            )
            query_raw = part if query_raw is None else query_raw + part
        queries = norm_rows(query_raw.reshape(rows, width_q // HD, HD), query_gain[0]).astype(
            jnp.bfloat16
        )
        present = lower + jnp.arange(rows) < lengths[0, 0]

        def forward(keys_in, values_in):
            return attend(queries, keys_in, values_in, key_gain[0], usable, present, cross_gate[0])

        context, pullback = jax.vjp(forward, keys_raw, values_raw)
        contexts.append(context.astype(jnp.bfloat16))
        key_part, value_part = pullback(context_grad[0, 0, lower : lower + rows].astype(jnp.float32))
        key_back = key_part if key_back is None else key_back + key_part
        value_back = value_part if value_back is None else value_back + value_part
        if chunk + 1 < chunks:
            gathered[chunk + 1], key_back, value_back = lax.optimization_barrier(
                (gathered[chunk + 1], key_back, value_back)
            )
    gated_context = jnp.concatenate(contexts, axis=0).reshape(1, 1, text_rows, width_q)
    key_flat = key_back.reshape(slot_rows, width_k).astype(jnp.bfloat16)
    value_flat = value_back.reshape(slot_rows, width_k).astype(jnp.bfloat16)

    contract = (((1,), (1,)), ((), ()))
    partial_sum = jnp.zeros((slot_rows, image.shape[1]), jnp.bfloat16)
    for code in key_blocks:
        term = lax.dot_general(key_flat, key_blocks[code], contract, preferred_element_type=jnp.float32)
        term = term + lax.dot_general(
            value_flat, value_blocks[code], contract, preferred_element_type=jnp.float32
        )
        partial_sum = lax.dynamic_update_slice_in_dim(
            partial_sum, term.astype(jnp.bfloat16), (dp_index ^ code) * block_rows, axis=1
        )
    summed = lax.psum_scatter(partial_sum, "mp", scatter_dimension=1, tiled=True)

    routed = summed
    for steps in range(1, sections):
        moved = shifted(summed, "section", steps)
        source = (section - steps) % sections
        routed = jnp.where(image_of[0, source] == section, moved, routed)
    vision_grad = routed.reshape(1, 1, slot_rows, part_width)

    inner = (((0,), (0,)), ((), ()))
    grad_blocks = {}
    for code in key_blocks:
        piece = columns_of(image, (dp_index ^ code) * block_rows, block_rows)
        key_part = lax.dot_general(piece, key_flat, inner, preferred_element_type=jnp.float32)
        value_part = lax.dot_general(piece, value_flat, inner, preferred_element_type=jnp.float32)
        grad_blocks[code] = jnp.concatenate(
            [key_part.astype(jnp.bfloat16), value_part.astype(jnp.bfloat16)], axis=1
        )
    both_grads = scatter_blocks(grad_blocks, "dp").astype(jnp.bfloat16)
    key_weight_grad = both_grads[:, :width_k][None]
    value_weight_grad = both_grads[:, width_k:][None]
    return (gated_context, vision_grad, key_weight_grad, value_weight_grad)


def solution(mesh):
    return jax.shard_map(
        per_device,
        mesh=mesh,
        in_specs=(
            P("dp", "section", None, "mp"),
            P("dp", "section", None, "mp"),
            P("dp", None),
            P("dp", "section"),
            P("dp", None),
            P("section", None),
            P("section", "dp", "mp"),
            P("section", "dp", "mp"),
            P("section", "dp", "mp"),
            P("section", None),
            P("section", None),
            P("section"),
            P("dp", "section", None, "mp"),
        ),
        out_specs=(
            P("dp", "section", None, "mp"),
            P("dp", "section", None, "mp"),
            P("section", "dp", "mp"),
            P("section", "dp", "mp"),
        ),
        check_vma=False,
    )
```

```python
import jax
import jax.numpy as jnp
from jax import lax
from jax.sharding import PartitionSpec as P

HD = 128
TILE_ROWS = 64


def shifted(value, axis, steps):
    count = lax.axis_size(axis)
    pairs = [(source, (source + steps) % count) for source in range(count)]
    return lax.ppermute(value, axis, pairs)


def swapped(value, axis, mask):
    count = lax.axis_size(axis)
    pairs = [(source, source ^ mask) for source in range(count)]
    return lax.ppermute(value, axis, pairs)


def bit_order(count, high_first):
    bits = []
    step = 1
    while step < count:
        bits.append(step)
        step *= 2
    return bits[::-1] if high_first else bits


def gather_blocks(block, axis):
    count = lax.axis_size(axis)
    held = {0: block}
    for mask in bit_order(count, True):
        codes = sorted(held)
        arrived = swapped(jnp.stack([held[c] for c in codes]), axis, mask)
        for position, code in enumerate(codes):
            held[code ^ mask] = arrived[position]
    return held


def scatter_blocks(by_code, axis):
    count = lax.axis_size(axis)
    held = {code: value.astype(jnp.float32) for code, value in by_code.items()}
    for mask in bit_order(count, False):
        sent = sorted(c for c in held if c & mask)
        kept = [c ^ mask for c in sent]
        arrived = swapped(jnp.stack([held[c].astype(jnp.bfloat16) for c in sent]), axis, mask)
        held = {c: held[c] + arrived[position].astype(jnp.float32) for position, c in enumerate(kept)}
    return held[0]


def norm_rows(values, gain):
    values = values.astype(jnp.float32)
    scaled = values * lax.rsqrt(jnp.mean(values * values, axis=-1, keepdims=True) + 1e-05)
    return scaled * gain


def rounded(values):
    return lax.optimization_barrier(values.astype(jnp.bfloat16)).astype(jnp.float32)


def attend(queries, keys_raw, values_raw, key_norm, usable, present, gate_value):
    keys = rounded(norm_rows(keys_raw, key_norm))
    values = rounded(values_raw)
    text_rows, heads, depth = queries.shape
    groups = keys.shape[1]
    grouped = queries.astype(jnp.float32).reshape(text_rows, groups, heads // groups, depth)
    scores = jnp.einsum("tgjd,vgd->gjtv", grouped, keys) * depth ** (-0.5)
    scores = jnp.where(usable[None, None, None, :], scores, -1e30)
    highest = lax.stop_gradient(jnp.max(scores, axis=-1, keepdims=True))
    weights = jnp.exp(scores - highest)
    probs = rounded(weights / jnp.sum(weights, axis=-1, keepdims=True))
    context = jnp.einsum("gjtv,vgd->tgjd", probs, values).reshape(text_rows, heads * depth)
    return jnp.where(present[:, None], jnp.tanh(gate_value) * context, 0.0)


def columns_of(values, start, width):
    return lax.dynamic_slice_in_dim(values, start, width, axis=1)


def per_device(
    text_in,
    vision,
    tile_counts,
    lengths,
    image_of,
    norm_gain,
    query_weight,
    key_weight,
    value_weight,
    query_gain,
    key_gain,
    cross_gate,
    context_grad,
):
    sections = lax.axis_size("section")
    section = lax.axis_index("section")
    dp_index = lax.axis_index("dp")
    block_rows = query_weight.shape[1]

    query_blocks = gather_blocks(query_weight[0], "dp")
    key_blocks = gather_blocks(key_weight[0], "dp")
    value_blocks = gather_blocks(value_weight[0], "dp")

    slot_rows = vision.shape[2]
    part_width = vision.shape[3]
    wanted = image_of[0, section]
    image_part = vision[0, 0]
    for steps in range(1, sections):
        moved = shifted(vision, "section", steps)[0, 0]
        image_part = jnp.where((section - steps) % sections == wanted, moved, image_part)
    image = lax.all_gather(image_part, "mp", axis=1, tiled=True)

    width_k = key_weight.shape[2]
    keys_raw = None
    values_raw = None
    for code in key_blocks:
        piece = columns_of(image, (dp_index ^ code) * block_rows, block_rows)
        key_part = jnp.dot(piece, key_blocks[code], preferred_element_type=jnp.float32)
        value_part = jnp.dot(piece, value_blocks[code], preferred_element_type=jnp.float32)
        keys_raw = key_part if keys_raw is None else keys_raw + key_part
        values_raw = value_part if values_raw is None else values_raw + value_part
    keys_raw = keys_raw.reshape(slot_rows, width_k // HD, HD)
    values_raw = values_raw.reshape(slot_rows, width_k // HD, HD)
    usable = jnp.arange(slot_rows) < tile_counts[0, wanted] * TILE_ROWS

    arrived = shifted(text_in, "section", 1)
    text_rows = text_in.shape[2]
    width_q = query_weight.shape[2]
    if text_rows % 64 == 0:
        bounds = [0, text_rows * 5 // 8, text_rows]
    else:
        bounds = [0, text_rows]
    chunks = len(bounds) - 1
    contexts = []
    key_back = None
    value_back = None
    gathered = [
        lax.all_gather(arrived[:, :, bounds[chunk] : bounds[chunk + 1]], "mp", axis=3, tiled=True)
        for chunk in range(chunks)
    ]
    for chunk in range(chunks):
        lower = bounds[chunk]
        rows = bounds[chunk + 1] - lower
        full_text = gathered[chunk][0, 0]
        normed = norm_rows(full_text, norm_gain[0]).astype(jnp.bfloat16)
        query_raw = None
        for code, block in query_blocks.items():
            part = jnp.dot(
                columns_of(normed, (dp_index ^ code) * block_rows, block_rows),
                block,
                preferred_element_type=jnp.float32,
            )
            query_raw = part if query_raw is None else query_raw + part
        queries = norm_rows(query_raw.reshape(rows, width_q // HD, HD), query_gain[0]).astype(
            jnp.bfloat16
        )
        present = lower + jnp.arange(rows) < lengths[0, 0]

        def forward(keys_in, values_in):
            return attend(queries, keys_in, values_in, key_gain[0], usable, present, cross_gate[0])

        context, pullback = jax.vjp(forward, keys_raw, values_raw)
        contexts.append(context.astype(jnp.bfloat16))
        key_part, value_part = pullback(context_grad[0, 0, lower : lower + rows].astype(jnp.float32))
        key_back = key_part if key_back is None else key_back + key_part
        value_back = value_part if value_back is None else value_back + value_part
        if chunk + 1 < chunks:
            gathered[chunk + 1], key_back, value_back = lax.optimization_barrier(
                (gathered[chunk + 1], key_back, value_back)
            )
    gated_context = jnp.concatenate(contexts, axis=0).reshape(1, 1, text_rows, width_q)
    key_flat = key_back.reshape(slot_rows, width_k).astype(jnp.bfloat16)
    value_flat = value_back.reshape(slot_rows, width_k).astype(jnp.bfloat16)

    contract = (((1,), (1,)), ((), ()))
    partial_sum = jnp.zeros((slot_rows, image.shape[1]), jnp.bfloat16)
    for code in key_blocks:
        term = lax.dot_general(key_flat, key_blocks[code], contract, preferred_element_type=jnp.float32)
        term = term + lax.dot_general(
            value_flat, value_blocks[code], contract, preferred_element_type=jnp.float32
        )
        partial_sum = lax.dynamic_update_slice_in_dim(
            partial_sum, term.astype(jnp.bfloat16), (dp_index ^ code) * block_rows, axis=1
        )
    summed = lax.psum_scatter(partial_sum, "mp", scatter_dimension=1, tiled=True)

    routed = summed
    for steps in range(1, sections):
        moved = shifted(summed, "section", steps)
        source = (section - steps) % sections
        routed = jnp.where(image_of[0, source] == section, moved, routed)
    vision_grad = routed.reshape(1, 1, slot_rows, part_width)

    inner = (((0,), (0,)), ((), ()))
    grad_blocks = {}
    for code in key_blocks:
        piece = columns_of(image, (dp_index ^ code) * block_rows, block_rows)
        key_part = lax.dot_general(piece, key_flat, inner, preferred_element_type=jnp.float32)
        value_part = lax.dot_general(piece, value_flat, inner, preferred_element_type=jnp.float32)
        grad_blocks[code] = jnp.concatenate(
            [key_part.astype(jnp.bfloat16), value_part.astype(jnp.bfloat16)], axis=1
        )
    both_grads = scatter_blocks(grad_blocks, "dp").astype(jnp.bfloat16)
    key_weight_grad = both_grads[:, :width_k][None]
    value_weight_grad = both_grads[:, width_k:][None]
    return (gated_context, vision_grad, key_weight_grad, value_weight_grad)


def solution(mesh):
    return jax.shard_map(
        per_device,
        mesh=mesh,
        in_specs=(
            P("dp", "section", None, "mp"),
            P("dp", "section", None, "mp"),
            P("dp", None),
            P("dp", "section"),
            P("dp", None),
            P("section", None),
            P("section", "dp", "mp"),
            P("section", "dp", "mp"),
            P("section", "dp", "mp"),
            P("section", None),
            P("section", None),
            P("section"),
            P("dp", "section", None, "mp"),
        ),
        out_specs=(
            P("dp", "section", None, "mp"),
            P("dp", "section", None, "mp"),
            P("section", "dp", "mp"),
            P("section", "dp", "mp"),
        ),
        check_vma=False,
    )
```

```python
import jax
import jax.numpy as jnp
from jax import lax
from jax.sharding import PartitionSpec as P

HD = 128
TILE_ROWS = 64


def shifted(value, axis, steps):
    count = lax.axis_size(axis)
    pairs = [(source, (source + steps) % count) for source in range(count)]
    return lax.ppermute(value, axis, pairs)


def swapped(value, axis, mask):
    count = lax.axis_size(axis)
    pairs = [(source, source ^ mask) for source in range(count)]
    return lax.ppermute(value, axis, pairs)


def bit_order(count, high_first):
    bits = []
    step = 1
    while step < count:
        bits.append(step)
        step *= 2
    return bits[::-1] if high_first else bits


def gather_blocks(block, axis):
    count = lax.axis_size(axis)
    held = {0: block}
    for mask in bit_order(count, True):
        codes = sorted(held)
        arrived = swapped(jnp.stack([held[c] for c in codes]), axis, mask)
        for position, code in enumerate(codes):
            held[code ^ mask] = arrived[position]
    return held


def gather_groups(block, axis):
    count = lax.axis_size(axis)
    codes = [0]
    stack = block[None]
    groups = [(codes, stack)]
    for mask in bit_order(count, True):
        arrived = swapped(stack, axis, mask)
        moved = [code ^ mask for code in codes]
        groups = [(codes, stack), (moved, arrived)]
        stack = jnp.concatenate([stack, arrived], axis=0)
        codes = codes + moved
    return groups


def code_slices(values, index, codes, width):
    pieces = [lax.dynamic_slice_in_dim(values, (index ^ code) * width, width, axis=1) for code in codes]
    return pieces[0] if len(pieces) == 1 else jnp.concatenate(pieces, axis=1)


def flat(stack):
    return stack.reshape(stack.shape[0] * stack.shape[1], stack.shape[2])


def scatter_blocks(by_code, axis):
    count = lax.axis_size(axis)
    held = {code: value.astype(jnp.float32) for code, value in by_code.items()}
    for mask in bit_order(count, False):
        sent = sorted(c for c in held if c & mask)
        kept = [c ^ mask for c in sent]
        arrived = swapped(jnp.stack([held[c].astype(jnp.bfloat16) for c in sent]), axis, mask)
        held = {c: held[c] + arrived[position].astype(jnp.float32) for position, c in enumerate(kept)}
    return held[0]


def norm_rows(values, gain):
    values = values.astype(jnp.float32)
    scaled = values * lax.rsqrt(jnp.mean(values * values, axis=-1, keepdims=True) + 1e-05)
    return scaled * gain


def rounded(values):
    return lax.optimization_barrier(values.astype(jnp.bfloat16)).astype(jnp.float32)


def attend(queries, keys_raw, values_raw, key_norm, usable, present, gate_value):
    keys = rounded(norm_rows(keys_raw, key_norm))
    values = rounded(values_raw)
    text_rows, heads, depth = queries.shape
    groups = keys.shape[1]
    grouped = queries.astype(jnp.float32).reshape(text_rows, groups, heads // groups, depth)
    scores = jnp.einsum("tgjd,vgd->gjtv", grouped, keys) * depth ** (-0.5)
    scores = jnp.where(usable[None, None, None, :], scores, -1e30)
    highest = lax.stop_gradient(jnp.max(scores, axis=-1, keepdims=True))
    weights = jnp.exp(scores - highest)
    probs = rounded(weights / jnp.sum(weights, axis=-1, keepdims=True))
    context = jnp.einsum("gjtv,vgd->tgjd", probs, values).reshape(text_rows, heads * depth)
    return jnp.where(present[:, None], jnp.tanh(gate_value) * context, 0.0)


def columns_of(values, start, width):
    return lax.dynamic_slice_in_dim(values, start, width, axis=1)


def per_device(
    text_in,
    vision,
    tile_counts,
    lengths,
    image_of,
    norm_gain,
    query_weight,
    key_weight,
    value_weight,
    query_gain,
    key_gain,
    cross_gate,
    context_grad,
):
    sections = lax.axis_size("section")
    section = lax.axis_index("section")
    dp_index = lax.axis_index("dp")
    block_rows = query_weight.shape[1]

    dp_count = lax.axis_size("dp")
    query_groups = gather_groups(query_weight[0], "dp")
    key_groups = gather_groups(key_weight[0], "dp")
    value_groups = gather_groups(value_weight[0], "dp")

    slot_rows = vision.shape[2]
    part_width = vision.shape[3]
    wanted = image_of[0, section]
    image_part = vision[0, 0]
    for steps in range(1, sections):
        moved = shifted(vision, "section", steps)[0, 0]
        image_part = jnp.where((section - steps) % sections == wanted, moved, image_part)
    image = lax.all_gather(image_part, "mp", axis=1, tiled=True)

    width_k = key_weight.shape[2]
    keys_raw = None
    values_raw = None
    for (codes, key_stack), (_, value_stack) in zip(key_groups, value_groups):
        piece = code_slices(image, dp_index, codes, block_rows)
        key_part = jnp.dot(piece, flat(key_stack), preferred_element_type=jnp.float32)
        value_part = jnp.dot(piece, flat(value_stack), preferred_element_type=jnp.float32)
        keys_raw = key_part if keys_raw is None else keys_raw + key_part
        values_raw = value_part if values_raw is None else values_raw + value_part
    keys_raw = keys_raw.reshape(slot_rows, width_k // HD, HD)
    values_raw = values_raw.reshape(slot_rows, width_k // HD, HD)
    usable = jnp.arange(slot_rows) < tile_counts[0, wanted] * TILE_ROWS

    arrived = shifted(text_in, "section", 1)
    text_rows = text_in.shape[2]
    width_q = query_weight.shape[2]
    chunks = 2 if text_rows % 16 == 0 else 1
    rows = text_rows // chunks
    contexts = []
    key_back = None
    value_back = None
    gathered = [
        lax.all_gather(arrived[:, :, chunk * rows : (chunk + 1) * rows], "mp", axis=3, tiled=True)
        for chunk in range(chunks)
    ]
    for chunk in range(chunks):
        lower = chunk * rows
        full_text = gathered[chunk][0, 0]
        normed = norm_rows(full_text, norm_gain[0]).astype(jnp.bfloat16)
        query_raw = None
        for codes, stack in query_groups:
            part = jnp.dot(
                code_slices(normed, dp_index, codes, block_rows),
                flat(stack),
                preferred_element_type=jnp.float32,
            )
            query_raw = part if query_raw is None else query_raw + part
        queries = norm_rows(query_raw.reshape(rows, width_q // HD, HD), query_gain[0]).astype(
            jnp.bfloat16
        )
        present = lower + jnp.arange(rows) < lengths[0, 0]

        def forward(keys_in, values_in):
            return attend(queries, keys_in, values_in, key_gain[0], usable, present, cross_gate[0])

        context, pullback = jax.vjp(forward, keys_raw, values_raw)
        contexts.append(context.astype(jnp.bfloat16))
        key_part, value_part = pullback(context_grad[0, 0, lower : lower + rows].astype(jnp.float32))
        key_back = key_part if key_back is None else key_back + key_part
        value_back = value_part if value_back is None else value_back + value_part
        if chunk + 1 < chunks:
            gathered[chunk + 1], key_back, value_back = lax.optimization_barrier(
                (gathered[chunk + 1], key_back, value_back)
            )
    gated_context = jnp.concatenate(contexts, axis=0).reshape(1, 1, text_rows, width_q)
    key_flat = key_back.reshape(slot_rows, width_k).astype(jnp.bfloat16)
    value_flat = value_back.reshape(slot_rows, width_k).astype(jnp.bfloat16)

    contract = (((1,), (1,)), ((), ()))
    by_code = {}
    for (codes, key_stack), (_, value_stack) in zip(key_groups, value_groups):
        term = lax.dot_general(key_flat, flat(key_stack), contract, preferred_element_type=jnp.float32)
        term = term + lax.dot_general(
            value_flat, flat(value_stack), contract, preferred_element_type=jnp.float32
        )
        term = term.astype(jnp.bfloat16)
        for position, code in enumerate(codes):
            by_code[code] = term[:, position * block_rows : (position + 1) * block_rows]
    in_code_order = jnp.concatenate([by_code[code] for code in range(dp_count)], axis=1)
    partial_sum = code_slices(in_code_order, dp_index, list(range(dp_count)), block_rows)
    summed = lax.psum_scatter(partial_sum, "mp", scatter_dimension=1, tiled=True)

    routed = summed
    for steps in range(1, sections):
        moved = shifted(summed, "section", steps)
        source = (section - steps) % sections
        routed = jnp.where(image_of[0, source] == section, moved, routed)
    vision_grad = routed.reshape(1, 1, slot_rows, part_width)

    inner = (((0,), (0,)), ((), ()))
    grad_blocks = {}
    for codes, _ in key_groups:
        piece = code_slices(image, dp_index, codes, block_rows)
        key_part = lax.dot_general(piece, key_flat, inner, preferred_element_type=jnp.float32)
        value_part = lax.dot_general(piece, value_flat, inner, preferred_element_type=jnp.float32)
        both = jnp.concatenate([key_part.astype(jnp.bfloat16), value_part.astype(jnp.bfloat16)], axis=1)
        for position, code in enumerate(codes):
            grad_blocks[code] = both[position * block_rows : (position + 1) * block_rows]
    both_grads = scatter_blocks(grad_blocks, "dp").astype(jnp.bfloat16)
    key_weight_grad = both_grads[:, :width_k][None]
    value_weight_grad = both_grads[:, width_k:][None]
    return (gated_context, vision_grad, key_weight_grad, value_weight_grad)


def solution(mesh):
    return jax.shard_map(
        per_device,
        mesh=mesh,
        in_specs=(
            P("dp", "section", None, "mp"),
            P("dp", "section", None, "mp"),
            P("dp", None),
            P("dp", "section"),
            P("dp", None),
            P("section", None),
            P("section", "dp", "mp"),
            P("section", "dp", "mp"),
            P("section", "dp", "mp"),
            P("section", None),
            P("section", None),
            P("section"),
            P("dp", "section", None, "mp"),
        ),
        out_specs=(
            P("dp", "section", None, "mp"),
            P("dp", "section", None, "mp"),
            P("section", "dp", "mp"),
            P("section", "dp", "mp"),
        ),
        check_vma=False,
    )
```

```python
import jax
import jax.numpy as jnp
from jax import lax
from jax.sharding import PartitionSpec as P

HD = 128
TILE_ROWS = 64


def shifted(value, axis, steps):
    count = lax.axis_size(axis)
    pairs = [(source, (source + steps) % count) for source in range(count)]
    return lax.ppermute(value, axis, pairs)


def swapped(value, axis, mask):
    count = lax.axis_size(axis)
    pairs = [(source, source ^ mask) for source in range(count)]
    return lax.ppermute(value, axis, pairs)


def bit_order(count, high_first):
    bits = []
    step = 1
    while step < count:
        bits.append(step)
        step *= 2
    return bits[::-1] if high_first else bits


def gather_blocks(block, axis):
    count = lax.axis_size(axis)
    held = {0: block}
    for mask in bit_order(count, True):
        codes = sorted(held)
        arrived = swapped(jnp.stack([held[c] for c in codes]), axis, mask)
        for position, code in enumerate(codes):
            held[code ^ mask] = arrived[position]
    return held


def scatter_blocks(by_code, axis):
    count = lax.axis_size(axis)
    held = {code: value.astype(jnp.float32) for code, value in by_code.items()}
    for mask in bit_order(count, False):
        sent = sorted(c for c in held if c & mask)
        kept = [c ^ mask for c in sent]
        arrived = swapped(jnp.stack([held[c].astype(jnp.bfloat16) for c in sent]), axis, mask)
        held = {c: held[c] + arrived[position].astype(jnp.float32) for position, c in enumerate(kept)}
    return held[0]


def norm_rows(values, gain):
    values = values.astype(jnp.float32)
    scaled = values * lax.rsqrt(jnp.mean(values * values, axis=-1, keepdims=True) + 1e-05)
    return scaled * gain


def rounded(values):
    return lax.optimization_barrier(values.astype(jnp.bfloat16)).astype(jnp.float32)


def attend(queries, keys_raw, values_raw, key_norm, usable, present, gate_value):
    keys = rounded(norm_rows(keys_raw, key_norm))
    values = rounded(values_raw)
    text_rows, heads, depth = queries.shape
    groups = keys.shape[1]
    grouped = queries.astype(jnp.float32).reshape(text_rows, groups, heads // groups, depth)
    scores = jnp.einsum("tgjd,vgd->gjtv", grouped, keys) * depth ** (-0.5)
    scores = jnp.where(usable[None, None, None, :], scores, -1e30)
    highest = lax.stop_gradient(jnp.max(scores, axis=-1, keepdims=True))
    weights = jnp.exp(scores - highest)
    probs = rounded(weights / jnp.sum(weights, axis=-1, keepdims=True))
    context = jnp.einsum("gjtv,vgd->tgjd", probs, values).reshape(text_rows, heads * depth)
    return jnp.where(present[:, None], jnp.tanh(gate_value) * context, 0.0)


def columns_of(values, start, width):
    return lax.dynamic_slice_in_dim(values, start, width, axis=1)


def per_device(
    text_in,
    vision,
    tile_counts,
    lengths,
    image_of,
    norm_gain,
    query_weight,
    key_weight,
    value_weight,
    query_gain,
    key_gain,
    cross_gate,
    context_grad,
):
    sections = lax.axis_size("section")
    section = lax.axis_index("section")
    dp_index = lax.axis_index("dp")
    block_rows = query_weight.shape[1]

    query_blocks = gather_blocks(query_weight[0], "dp")
    key_blocks = gather_blocks(key_weight[0], "dp")
    value_blocks = gather_blocks(value_weight[0], "dp")

    slot_rows = vision.shape[2]
    part_width = vision.shape[3]
    wanted = image_of[0, section]
    halves = 2 if slot_rows % 16 == 0 else 1
    half_rows = slot_rows // halves
    image_halves = []
    for half in range(halves):
        local = vision[:, :, half * half_rows : (half + 1) * half_rows]
        image_part = local[0, 0]
        for steps in range(1, sections):
            moved = shifted(local, "section", steps)[0, 0]
            image_part = jnp.where((section - steps) % sections == wanted, moved, image_part)
        image_halves.append(lax.all_gather(image_part, "mp", axis=1, tiled=True))
    image = image_halves[0] if halves == 1 else jnp.concatenate(image_halves, axis=0)

    width_k = key_weight.shape[2]
    keys_raw = None
    values_raw = None
    for code in key_blocks:
        piece = columns_of(image, (dp_index ^ code) * block_rows, block_rows)
        key_part = jnp.dot(piece, key_blocks[code], preferred_element_type=jnp.float32)
        value_part = jnp.dot(piece, value_blocks[code], preferred_element_type=jnp.float32)
        keys_raw = key_part if keys_raw is None else keys_raw + key_part
        values_raw = value_part if values_raw is None else values_raw + value_part
    keys_raw = keys_raw.reshape(slot_rows, width_k // HD, HD)
    values_raw = values_raw.reshape(slot_rows, width_k // HD, HD)
    usable = jnp.arange(slot_rows) < tile_counts[0, wanted] * TILE_ROWS

    arrived = shifted(text_in, "section", 1)
    text_rows = text_in.shape[2]
    width_q = query_weight.shape[2]
    chunks = 2 if text_rows % 16 == 0 else 1
    rows = text_rows // chunks
    contexts = []
    key_back = None
    value_back = None
    gathered = [
        lax.all_gather(arrived[:, :, chunk * rows : (chunk + 1) * rows], "mp", axis=3, tiled=True)
        for chunk in range(chunks)
    ]
    for chunk in range(chunks):
        lower = chunk * rows
        full_text = gathered[chunk][0, 0]
        normed = norm_rows(full_text, norm_gain[0]).astype(jnp.bfloat16)
        query_raw = None
        for code, block in query_blocks.items():
            part = jnp.dot(
                columns_of(normed, (dp_index ^ code) * block_rows, block_rows),
                block,
                preferred_element_type=jnp.float32,
            )
            query_raw = part if query_raw is None else query_raw + part
        queries = norm_rows(query_raw.reshape(rows, width_q // HD, HD), query_gain[0]).astype(
            jnp.bfloat16
        )
        present = lower + jnp.arange(rows) < lengths[0, 0]

        def forward(keys_in, values_in):
            return attend(queries, keys_in, values_in, key_gain[0], usable, present, cross_gate[0])

        context, pullback = jax.vjp(forward, keys_raw, values_raw)
        contexts.append(context.astype(jnp.bfloat16))
        key_part, value_part = pullback(context_grad[0, 0, lower : lower + rows].astype(jnp.float32))
        key_back = key_part if key_back is None else key_back + key_part
        value_back = value_part if value_back is None else value_back + value_part
        if chunk + 1 < chunks:
            gathered[chunk + 1], key_back, value_back = lax.optimization_barrier(
                (gathered[chunk + 1], key_back, value_back)
            )
    gated_context = jnp.concatenate(contexts, axis=0).reshape(1, 1, text_rows, width_q)
    key_flat = key_back.reshape(slot_rows, width_k).astype(jnp.bfloat16)
    value_flat = value_back.reshape(slot_rows, width_k).astype(jnp.bfloat16)

    contract = (((1,), (1,)), ((), ()))
    partial_sum = jnp.zeros((slot_rows, image.shape[1]), jnp.bfloat16)
    for code in key_blocks:
        term = lax.dot_general(key_flat, key_blocks[code], contract, preferred_element_type=jnp.float32)
        term = term + lax.dot_general(
            value_flat, value_blocks[code], contract, preferred_element_type=jnp.float32
        )
        partial_sum = lax.dynamic_update_slice_in_dim(
            partial_sum, term.astype(jnp.bfloat16), (dp_index ^ code) * block_rows, axis=1
        )
    summed = lax.psum_scatter(partial_sum, "mp", scatter_dimension=1, tiled=True)

    routed = summed
    for steps in range(1, sections):
        moved = shifted(summed, "section", steps)
        source = (section - steps) % sections
        routed = jnp.where(image_of[0, source] == section, moved, routed)
    vision_grad = routed.reshape(1, 1, slot_rows, part_width)

    inner = (((0,), (0,)), ((), ()))
    grad_blocks = {}
    for code in key_blocks:
        piece = columns_of(image, (dp_index ^ code) * block_rows, block_rows)
        key_part = lax.dot_general(piece, key_flat, inner, preferred_element_type=jnp.float32)
        value_part = lax.dot_general(piece, value_flat, inner, preferred_element_type=jnp.float32)
        grad_blocks[code] = jnp.concatenate(
            [key_part.astype(jnp.bfloat16), value_part.astype(jnp.bfloat16)], axis=1
        )
    both_grads = scatter_blocks(grad_blocks, "dp").astype(jnp.bfloat16)
    key_weight_grad = both_grads[:, :width_k][None]
    value_weight_grad = both_grads[:, width_k:][None]
    return (gated_context, vision_grad, key_weight_grad, value_weight_grad)


def solution(mesh):
    return jax.shard_map(
        per_device,
        mesh=mesh,
        in_specs=(
            P("dp", "section", None, "mp"),
            P("dp", "section", None, "mp"),
            P("dp", None),
            P("dp", "section"),
            P("dp", None),
            P("section", None),
            P("section", "dp", "mp"),
            P("section", "dp", "mp"),
            P("section", "dp", "mp"),
            P("section", None),
            P("section", None),
            P("section"),
            P("dp", "section", None, "mp"),
        ),
        out_specs=(
            P("dp", "section", None, "mp"),
            P("dp", "section", None, "mp"),
            P("section", "dp", "mp"),
            P("section", "dp", "mp"),
        ),
        check_vma=False,
    )
```

```python
import jax
import jax.numpy as jnp
from jax import lax
from jax.sharding import PartitionSpec as P

HD = 128
TILE_ROWS = 64


def shifted(value, axis, steps):
    count = lax.axis_size(axis)
    pairs = [(source, (source + steps) % count) for source in range(count)]
    return lax.ppermute(value, axis, pairs)


def swapped(value, axis, mask):
    count = lax.axis_size(axis)
    pairs = [(source, source ^ mask) for source in range(count)]
    return lax.ppermute(value, axis, pairs)


def bit_order(count, high_first):
    bits = []
    step = 1
    while step < count:
        bits.append(step)
        step *= 2
    return bits[::-1] if high_first else bits


def gather_blocks(block, axis):
    count = lax.axis_size(axis)
    held = {0: block}
    for mask in bit_order(count, True):
        codes = sorted(held)
        arrived = swapped(jnp.stack([held[c] for c in codes]), axis, mask)
        for position, code in enumerate(codes):
            held[code ^ mask] = arrived[position]
    return held


def gather_groups(block, axis):
    count = lax.axis_size(axis)
    codes = [0]
    stack = block[None]
    groups = [(codes, stack)]
    for mask in bit_order(count, True):
        arrived = swapped(stack, axis, mask)
        moved = [code ^ mask for code in codes]
        groups = [(codes, stack), (moved, arrived)]
        stack = jnp.concatenate([stack, arrived], axis=0)
        codes = codes + moved
    return groups


def code_slices(values, index, codes, width):
    pieces = [lax.dynamic_slice_in_dim(values, (index ^ code) * width, width, axis=1) for code in codes]
    return pieces[0] if len(pieces) == 1 else jnp.concatenate(pieces, axis=1)


def flat(stack, start, width):
    return stack[:, :, start : start + width].reshape(stack.shape[0] * stack.shape[1], width)


def scatter_blocks(by_code, axis):
    count = lax.axis_size(axis)
    held = {code: value.astype(jnp.float32) for code, value in by_code.items()}
    for mask in bit_order(count, False):
        sent = sorted(c for c in held if c & mask)
        kept = [c ^ mask for c in sent]
        arrived = swapped(jnp.stack([held[c].astype(jnp.bfloat16) for c in sent]), axis, mask)
        held = {c: held[c] + arrived[position].astype(jnp.float32) for position, c in enumerate(kept)}
    return held[0]


def norm_rows(values, gain):
    values = values.astype(jnp.float32)
    scaled = values * lax.rsqrt(jnp.mean(values * values, axis=-1, keepdims=True) + 1e-05)
    return scaled * gain


def rounded(values):
    return lax.optimization_barrier(values.astype(jnp.bfloat16)).astype(jnp.float32)


def attend(queries, keys_raw, values_raw, key_norm, usable, present, gate_value):
    keys = rounded(norm_rows(keys_raw, key_norm))
    values = rounded(values_raw)
    text_rows, heads, depth = queries.shape
    groups = keys.shape[1]
    grouped = queries.astype(jnp.float32).reshape(text_rows, groups, heads // groups, depth)
    scores = jnp.einsum("tgjd,vgd->gjtv", grouped, keys) * depth ** (-0.5)
    scores = jnp.where(usable[None, None, None, :], scores, -1e30)
    highest = lax.stop_gradient(jnp.max(scores, axis=-1, keepdims=True))
    weights = jnp.exp(scores - highest)
    probs = rounded(weights / jnp.sum(weights, axis=-1, keepdims=True))
    context = jnp.einsum("gjtv,vgd->tgjd", probs, values).reshape(text_rows, heads * depth)
    return jnp.where(present[:, None], jnp.tanh(gate_value) * context, 0.0)


def columns_of(values, start, width):
    return lax.dynamic_slice_in_dim(values, start, width, axis=1)


def per_device(
    text_in,
    vision,
    tile_counts,
    lengths,
    image_of,
    norm_gain,
    query_weight,
    key_weight,
    value_weight,
    query_gain,
    key_gain,
    cross_gate,
    context_grad,
):
    sections = lax.axis_size("section")
    section = lax.axis_index("section")
    dp_index = lax.axis_index("dp")
    block_rows = query_weight.shape[1]

    dp_count = lax.axis_size("dp")
    width_q = query_weight.shape[2]
    width_k = key_weight.shape[2]
    weight_groups = gather_groups(
        jnp.concatenate([query_weight[0], key_weight[0], value_weight[0]], axis=1), "dp"
    )

    slot_rows = vision.shape[2]
    part_width = vision.shape[3]
    wanted = image_of[0, section]
    image_part = vision[0, 0]
    for steps in range(1, sections):
        moved = shifted(vision, "section", steps)[0, 0]
        image_part = jnp.where((section - steps) % sections == wanted, moved, image_part)
    image = lax.all_gather(image_part, "mp", axis=1, tiled=True)

    width_k = key_weight.shape[2]
    pair_raw = None
    for codes, stack in weight_groups:
        piece = code_slices(image, dp_index, codes, block_rows)
        part = jnp.dot(piece, flat(stack, width_q, 2 * width_k), preferred_element_type=jnp.float32)
        pair_raw = part if pair_raw is None else pair_raw + part
    keys_raw = pair_raw[:, :width_k]
    values_raw = pair_raw[:, width_k:]
    keys_raw = keys_raw.reshape(slot_rows, width_k // HD, HD)
    values_raw = values_raw.reshape(slot_rows, width_k // HD, HD)
    usable = jnp.arange(slot_rows) < tile_counts[0, wanted] * TILE_ROWS

    arrived = shifted(text_in, "section", 1)
    text_rows = text_in.shape[2]
    chunks = 2 if text_rows % 16 == 0 else 1
    rows = text_rows // chunks
    contexts = []
    key_back = None
    value_back = None
    gathered = [
        lax.all_gather(arrived[:, :, chunk * rows : (chunk + 1) * rows], "mp", axis=3, tiled=True)
        for chunk in range(chunks)
    ]
    for chunk in range(chunks):
        lower = chunk * rows
        full_text = gathered[chunk][0, 0]
        normed = norm_rows(full_text, norm_gain[0]).astype(jnp.bfloat16)
        query_raw = None
        for codes, stack in weight_groups:
            part = jnp.dot(
                code_slices(normed, dp_index, codes, block_rows),
                flat(stack, 0, width_q),
                preferred_element_type=jnp.float32,
            )
            query_raw = part if query_raw is None else query_raw + part
        queries = norm_rows(query_raw.reshape(rows, width_q // HD, HD), query_gain[0]).astype(
            jnp.bfloat16
        )
        present = lower + jnp.arange(rows) < lengths[0, 0]

        def forward(keys_in, values_in):
            return attend(queries, keys_in, values_in, key_gain[0], usable, present, cross_gate[0])

        context, pullback = jax.vjp(forward, keys_raw, values_raw)
        contexts.append(context.astype(jnp.bfloat16))
        key_part, value_part = pullback(context_grad[0, 0, lower : lower + rows].astype(jnp.float32))
        key_back = key_part if key_back is None else key_back + key_part
        value_back = value_part if value_back is None else value_back + value_part
        if chunk + 1 < chunks:
            gathered[chunk + 1], key_back, value_back = lax.optimization_barrier(
                (gathered[chunk + 1], key_back, value_back)
            )
    gated_context = jnp.concatenate(contexts, axis=0).reshape(1, 1, text_rows, width_q)
    key_flat = key_back.reshape(slot_rows, width_k).astype(jnp.bfloat16)
    value_flat = value_back.reshape(slot_rows, width_k).astype(jnp.bfloat16)

    contract = (((1,), (1,)), ((), ()))
    pair_flat = jnp.concatenate([key_flat, value_flat], axis=1)
    by_code = {}
    for codes, stack in weight_groups:
        term = lax.dot_general(
            pair_flat, flat(stack, width_q, 2 * width_k), contract, preferred_element_type=jnp.float32
        ).astype(jnp.bfloat16)
        for position, code in enumerate(codes):
            by_code[code] = term[:, position * block_rows : (position + 1) * block_rows]
    in_code_order = jnp.concatenate([by_code[code] for code in range(dp_count)], axis=1)
    partial_sum = code_slices(in_code_order, dp_index, list(range(dp_count)), block_rows)
    summed = lax.psum_scatter(partial_sum, "mp", scatter_dimension=1, tiled=True)

    routed = summed
    for steps in range(1, sections):
        moved = shifted(summed, "section", steps)
        source = (section - steps) % sections
        routed = jnp.where(image_of[0, source] == section, moved, routed)
    vision_grad = routed.reshape(1, 1, slot_rows, part_width)

    inner = (((0,), (0,)), ((), ()))
    grad_blocks = {}
    for codes, _ in weight_groups:
        piece = code_slices(image, dp_index, codes, block_rows)
        key_part = lax.dot_general(piece, key_flat, inner, preferred_element_type=jnp.float32)
        value_part = lax.dot_general(piece, value_flat, inner, preferred_element_type=jnp.float32)
        both = jnp.concatenate([key_part.astype(jnp.bfloat16), value_part.astype(jnp.bfloat16)], axis=1)
        for position, code in enumerate(codes):
            grad_blocks[code] = both[position * block_rows : (position + 1) * block_rows]
    both_grads = scatter_blocks(grad_blocks, "dp").astype(jnp.bfloat16)
    key_weight_grad = both_grads[:, :width_k][None]
    value_weight_grad = both_grads[:, width_k:][None]
    return (gated_context, vision_grad, key_weight_grad, value_weight_grad)


def solution(mesh):
    return jax.shard_map(
        per_device,
        mesh=mesh,
        in_specs=(
            P("dp", "section", None, "mp"),
            P("dp", "section", None, "mp"),
            P("dp", None),
            P("dp", "section"),
            P("dp", None),
            P("section", None),
            P("section", "dp", "mp"),
            P("section", "dp", "mp"),
            P("section", "dp", "mp"),
            P("section", None),
            P("section", None),
            P("section"),
            P("dp", "section", None, "mp"),
        ),
        out_specs=(
            P("dp", "section", None, "mp"),
            P("dp", "section", None, "mp"),
            P("section", "dp", "mp"),
            P("section", "dp", "mp"),
        ),
        check_vma=False,
    )
```

```python
import jax
import jax.numpy as jnp
from jax import lax
from jax.sharding import PartitionSpec as P

HD = 128
TILE_ROWS = 64


def shifted(value, axis, steps):
    count = lax.axis_size(axis)
    pairs = [(source, (source + steps) % count) for source in range(count)]
    return lax.ppermute(value, axis, pairs)


def swapped(value, axis, mask):
    count = lax.axis_size(axis)
    pairs = [(source, source ^ mask) for source in range(count)]
    return lax.ppermute(value, axis, pairs)


def bit_order(count, high_first):
    bits = []
    step = 1
    while step < count:
        bits.append(step)
        step *= 2
    return bits[::-1] if high_first else bits


def gather_blocks(block, axis):
    count = lax.axis_size(axis)
    held = {0: block}
    for mask in bit_order(count, True):
        codes = sorted(held)
        arrived = swapped(jnp.stack([held[c] for c in codes]), axis, mask)
        for position, code in enumerate(codes):
            held[code ^ mask] = arrived[position]
    return held


def scatter_blocks(by_code, axis):
    count = lax.axis_size(axis)
    held = {code: value.astype(jnp.float32) for code, value in by_code.items()}
    for mask in bit_order(count, False):
        sent = sorted(c for c in held if c & mask)
        kept = [c ^ mask for c in sent]
        arrived = swapped(jnp.stack([held[c].astype(jnp.bfloat16) for c in sent]), axis, mask)
        held = {c: held[c] + arrived[position].astype(jnp.float32) for position, c in enumerate(kept)}
    return held[0]


def norm_rows(values, gain):
    values = values.astype(jnp.float32)
    scaled = values * lax.rsqrt(jnp.mean(values * values, axis=-1, keepdims=True) + 1e-05)
    return scaled * gain


def rounded(values):
    return lax.optimization_barrier(values.astype(jnp.bfloat16)).astype(jnp.float32)


def attend(queries, keys_raw, values_raw, key_norm, usable, present, gate_value):
    keys = rounded(norm_rows(keys_raw, key_norm))
    values = rounded(values_raw)
    text_rows, heads, depth = queries.shape
    groups = keys.shape[1]
    grouped = queries.astype(jnp.float32).reshape(text_rows, groups, heads // groups, depth)
    scores = jnp.einsum("tgjd,vgd->gjtv", grouped, keys) * depth ** (-0.5)
    scores = jnp.where(usable[None, None, None, :], scores, -1e30)
    highest = lax.stop_gradient(jnp.max(scores, axis=-1, keepdims=True))
    weights = jnp.exp(scores - highest)
    probs = rounded(weights / jnp.sum(weights, axis=-1, keepdims=True))
    context = jnp.einsum("gjtv,vgd->tgjd", probs, values).reshape(text_rows, heads * depth)
    return jnp.where(present[:, None], jnp.tanh(gate_value) * context, 0.0)


def columns_of(values, start, width):
    return lax.dynamic_slice_in_dim(values, start, width, axis=1)


def per_device(
    text_in,
    vision,
    tile_counts,
    lengths,
    image_of,
    norm_gain,
    query_weight,
    key_weight,
    value_weight,
    query_gain,
    key_gain,
    cross_gate,
    context_grad,
):
    sections = lax.axis_size("section")
    section = lax.axis_index("section")
    dp_index = lax.axis_index("dp")
    block_rows = query_weight.shape[1]

    query_blocks = gather_blocks(query_weight[0], "dp")
    key_blocks = gather_blocks(key_weight[0], "dp")
    value_blocks = gather_blocks(value_weight[0], "dp")

    slot_rows = vision.shape[2]
    part_width = vision.shape[3]
    wanted = image_of[0, section]
    image_part = vision[0, 0]
    for steps in range(1, sections):
        moved = shifted(vision, "section", steps)[0, 0]
        image_part = jnp.where((section - steps) % sections == wanted, moved, image_part)
    image = lax.all_gather(image_part, "mp", axis=1, tiled=True)

    width_k = key_weight.shape[2]
    keys_raw = None
    values_raw = None
    for code in key_blocks:
        piece = columns_of(image, (dp_index ^ code) * block_rows, block_rows)
        key_part = jnp.dot(piece, key_blocks[code], preferred_element_type=jnp.float32)
        value_part = jnp.dot(piece, value_blocks[code], preferred_element_type=jnp.float32)
        keys_raw = key_part if keys_raw is None else keys_raw + key_part
        values_raw = value_part if values_raw is None else values_raw + value_part
    keys_raw = keys_raw.reshape(slot_rows, width_k // HD, HD)
    values_raw = values_raw.reshape(slot_rows, width_k // HD, HD)
    usable = jnp.arange(slot_rows) < tile_counts[0, wanted] * TILE_ROWS

    arrived = shifted(text_in, "section", 1)
    text_rows = text_in.shape[2]
    width_q = query_weight.shape[2]
    chunks = 2 if text_rows % 16 == 0 else 1
    rows = text_rows // chunks
    contexts = []
    key_back = None
    value_back = None
    gathered = [
        lax.all_gather(arrived[:, :, chunk * rows : (chunk + 1) * rows], "mp", axis=3, tiled=True)
        for chunk in range(chunks)
    ]
    for chunk in range(chunks):
        lower = chunk * rows
        full_text = gathered[chunk][0, 0]
        normed = norm_rows(full_text, norm_gain[0]).astype(jnp.bfloat16)
        query_raw = None
        for code, block in query_blocks.items():
            part = jnp.dot(
                columns_of(normed, (dp_index ^ code) * block_rows, block_rows),
                block,
                preferred_element_type=jnp.float32,
            )
            query_raw = part if query_raw is None else query_raw + part
        queries = norm_rows(query_raw.reshape(rows, width_q // HD, HD), query_gain[0]).astype(
            jnp.bfloat16
        )
        present = lower + jnp.arange(rows) < lengths[0, 0]

        def forward(keys_in, values_in):
            return attend(queries, keys_in, values_in, key_gain[0], usable, present, cross_gate[0])

        context, pullback = jax.vjp(forward, keys_raw, values_raw)
        contexts.append(context.astype(jnp.bfloat16))
        key_part, value_part = pullback(context_grad[0, 0, lower : lower + rows].astype(jnp.float32))
        key_back = key_part if key_back is None else key_back + key_part
        value_back = value_part if value_back is None else value_back + value_part
        if chunk + 1 < chunks:
            gathered[chunk + 1], key_back, value_back = lax.optimization_barrier(
                (gathered[chunk + 1], key_back, value_back)
            )
    gated_context = jnp.concatenate(contexts, axis=0).reshape(1, 1, text_rows, width_q)
    key_flat = key_back.reshape(slot_rows, width_k).astype(jnp.bfloat16)
    value_flat = value_back.reshape(slot_rows, width_k).astype(jnp.bfloat16)

    contract = (((1,), (1,)), ((), ()))
    partial_sum = jnp.zeros((slot_rows, image.shape[1]), jnp.bfloat16)
    for code in key_blocks:
        term = lax.dot_general(key_flat, key_blocks[code], contract, preferred_element_type=jnp.float32)
        term = term + lax.dot_general(
            value_flat, value_blocks[code], contract, preferred_element_type=jnp.float32
        )
        partial_sum = lax.dynamic_update_slice_in_dim(
            partial_sum, term.astype(jnp.bfloat16), (dp_index ^ code) * block_rows, axis=1
        )
    summed = lax.psum_scatter(partial_sum, "mp", scatter_dimension=1, tiled=True)

    routed = summed
    split = slot_rows // 2 if slot_rows % 16 == 0 else slot_rows
    for steps in range(1, sections):
        moved = [
            shifted(summed[lower : lower + split], "section", steps)
            for lower in range(0, slot_rows, split)
        ]
        moved = moved[0] if len(moved) == 1 else jnp.concatenate(moved, axis=0)
        source = (section - steps) % sections
        routed = jnp.where(image_of[0, source] == section, moved, routed)
    vision_grad = routed.reshape(1, 1, slot_rows, part_width)

    inner = (((0,), (0,)), ((), ()))
    grad_blocks = {}
    for code in key_blocks:
        piece = columns_of(image, (dp_index ^ code) * block_rows, block_rows)
        key_part = lax.dot_general(piece, key_flat, inner, preferred_element_type=jnp.float32)
        value_part = lax.dot_general(piece, value_flat, inner, preferred_element_type=jnp.float32)
        grad_blocks[code] = jnp.concatenate(
            [key_part.astype(jnp.bfloat16), value_part.astype(jnp.bfloat16)], axis=1
        )
    both_grads = scatter_blocks(grad_blocks, "dp").astype(jnp.bfloat16)
    key_weight_grad = both_grads[:, :width_k][None]
    value_weight_grad = both_grads[:, width_k:][None]
    return (gated_context, vision_grad, key_weight_grad, value_weight_grad)


def solution(mesh):
    return jax.shard_map(
        per_device,
        mesh=mesh,
        in_specs=(
            P("dp", "section", None, "mp"),
            P("dp", "section", None, "mp"),
            P("dp", None),
            P("dp", "section"),
            P("dp", None),
            P("section", None),
            P("section", "dp", "mp"),
            P("section", "dp", "mp"),
            P("section", "dp", "mp"),
            P("section", None),
            P("section", None),
            P("section"),
            P("dp", "section", None, "mp"),
        ),
        out_specs=(
            P("dp", "section", None, "mp"),
            P("dp", "section", None, "mp"),
            P("section", "dp", "mp"),
            P("section", "dp", "mp"),
        ),
        check_vma=False,
    )
```

```python
import jax
import jax.numpy as jnp
from jax import lax
from jax.sharding import PartitionSpec as P

HD = 128
TILE_ROWS = 64


def shifted(value, axis, steps):
    count = lax.axis_size(axis)
    pairs = [(source, (source + steps) % count) for source in range(count)]
    return lax.ppermute(value, axis, pairs)


def swapped(value, axis, mask):
    count = lax.axis_size(axis)
    pairs = [(source, source ^ mask) for source in range(count)]
    return lax.ppermute(value, axis, pairs)


def bit_order(count, high_first):
    bits = []
    step = 1
    while step < count:
        bits.append(step)
        step *= 2
    return bits[::-1] if high_first else bits


def gather_blocks(block, axis):
    count = lax.axis_size(axis)
    held = {0: block}
    for mask in bit_order(count, True):
        codes = sorted(held)
        arrived = swapped(jnp.stack([held[c] for c in codes]), axis, mask)
        for position, code in enumerate(codes):
            held[code ^ mask] = arrived[position]
    return held


def scatter_blocks(by_code, axis):
    count = lax.axis_size(axis)
    held = {code: value.astype(jnp.float32) for code, value in by_code.items()}
    for mask in bit_order(count, False):
        sent = sorted(c for c in held if c & mask)
        kept = [c ^ mask for c in sent]
        arrived = swapped(jnp.stack([held[c].astype(jnp.bfloat16) for c in sent]), axis, mask)
        held = {c: held[c] + arrived[position].astype(jnp.float32) for position, c in enumerate(kept)}
    return held[0]


def norm_rows(values, gain):
    values = values.astype(jnp.float32)
    scaled = values * lax.rsqrt(jnp.mean(values * values, axis=-1, keepdims=True) + 1e-05)
    return scaled * gain


def rounded(values):
    return lax.optimization_barrier(values.astype(jnp.bfloat16)).astype(jnp.float32)


def attend(queries, keys_raw, values_raw, key_norm, usable, present, gate_value):
    keys = rounded(norm_rows(keys_raw, key_norm))
    values = rounded(values_raw)
    text_rows, heads, depth = queries.shape
    groups = keys.shape[1]
    grouped = queries.astype(jnp.float32).reshape(text_rows, groups, heads // groups, depth)
    scores = jnp.einsum("tgjd,vgd->gjtv", grouped, keys) * depth ** (-0.5)
    scores = jnp.where(usable[None, None, None, :], scores, -1e30)
    highest = lax.stop_gradient(jnp.max(scores, axis=-1, keepdims=True))
    weights = jnp.exp(scores - highest)
    probs = rounded(weights / jnp.sum(weights, axis=-1, keepdims=True))
    context = jnp.einsum("gjtv,vgd->tgjd", probs, values).reshape(text_rows, heads * depth)
    return jnp.where(present[:, None], jnp.tanh(gate_value) * context, 0.0)


def columns_of(values, start, width):
    return lax.dynamic_slice_in_dim(values, start, width, axis=1)


def per_device(
    text_in,
    vision,
    tile_counts,
    lengths,
    image_of,
    norm_gain,
    query_weight,
    key_weight,
    value_weight,
    query_gain,
    key_gain,
    cross_gate,
    context_grad,
):
    sections = lax.axis_size("section")
    section = lax.axis_index("section")
    dp_index = lax.axis_index("dp")
    block_rows = query_weight.shape[1]

    query_blocks = gather_blocks(query_weight[0], "dp")
    key_blocks = gather_blocks(key_weight[0], "dp")
    value_blocks = gather_blocks(value_weight[0], "dp")

    slot_rows = vision.shape[2]
    part_width = vision.shape[3]
    wanted = image_of[0, section]
    image_part = vision[0, 0]
    for steps in range(1, sections):
        moved = shifted(vision, "section", steps)[0, 0]
        image_part = jnp.where((section - steps) % sections == wanted, moved, image_part)
    image = lax.all_gather(image_part, "mp", axis=1, tiled=True)

    width_k = key_weight.shape[2]
    keys_raw = None
    values_raw = None
    for code in key_blocks:
        piece = columns_of(image, (dp_index ^ code) * block_rows, block_rows)
        key_part = jnp.dot(piece, key_blocks[code], preferred_element_type=jnp.float32)
        value_part = jnp.dot(piece, value_blocks[code], preferred_element_type=jnp.float32)
        keys_raw = key_part if keys_raw is None else keys_raw + key_part
        values_raw = value_part if values_raw is None else values_raw + value_part
    keys_raw = keys_raw.reshape(slot_rows, width_k // HD, HD)
    values_raw = values_raw.reshape(slot_rows, width_k // HD, HD)
    usable = jnp.arange(slot_rows) < tile_counts[0, wanted] * TILE_ROWS

    arrived = shifted(text_in, "section", 1)
    text_rows = text_in.shape[2]
    width_q = query_weight.shape[2]
    chunks = 2 if text_rows % 16 == 0 else 1
    rows = text_rows // chunks
    contexts = []
    key_back = None
    value_back = None
    gathered = [
        lax.all_gather(arrived[:, :, chunk * rows : (chunk + 1) * rows], "mp", axis=3, tiled=True)
        for chunk in range(chunks)
    ]
    for chunk in range(chunks):
        lower = chunk * rows
        full_text = gathered[chunk][0, 0]
        normed = norm_rows(full_text, norm_gain[0]).astype(jnp.bfloat16)
        query_raw = None
        for code, block in query_blocks.items():
            part = jnp.dot(
                columns_of(normed, (dp_index ^ code) * block_rows, block_rows),
                block,
                preferred_element_type=jnp.float32,
            )
            query_raw = part if query_raw is None else query_raw + part
        queries = norm_rows(query_raw.reshape(rows, width_q // HD, HD), query_gain[0]).astype(
            jnp.bfloat16
        )
        present = lower + jnp.arange(rows) < lengths[0, 0]

        def forward(keys_in, values_in):
            return attend(queries, keys_in, values_in, key_gain[0], usable, present, cross_gate[0])

        context, pullback = jax.vjp(forward, keys_raw, values_raw)
        contexts.append(context.astype(jnp.bfloat16))
        key_part, value_part = pullback(context_grad[0, 0, lower : lower + rows].astype(jnp.float32))
        key_back = key_part if key_back is None else key_back + key_part
        value_back = value_part if value_back is None else value_back + value_part
        if chunk + 1 < chunks:
            gathered[chunk + 1], key_back, value_back = lax.optimization_barrier(
                (gathered[chunk + 1], key_back, value_back)
            )
    gated_context = jnp.concatenate(contexts, axis=0).reshape(1, 1, text_rows, width_q)
    key_flat = key_back.reshape(slot_rows, width_k).astype(jnp.bfloat16)
    value_flat = value_back.reshape(slot_rows, width_k).astype(jnp.bfloat16)

    contract = (((1,), (1,)), ((), ()))
    dp_count = lax.axis_size("dp")
    terms = []
    for code in range(dp_count):
        term = lax.dot_general(key_flat, key_blocks[code], contract, preferred_element_type=jnp.float32)
        term = term + lax.dot_general(
            value_flat, value_blocks[code], contract, preferred_element_type=jnp.float32
        )
        terms.append(term.astype(jnp.bfloat16))
    in_code_order = jnp.concatenate(terms, axis=1)
    partial_sum = jnp.concatenate(
        [columns_of(in_code_order, (dp_index ^ block) * block_rows, block_rows) for block in range(dp_count)],
        axis=1,
    )
    summed = lax.psum_scatter(partial_sum, "mp", scatter_dimension=1, tiled=True)

    routed = summed
    for steps in range(1, sections):
        moved = shifted(summed, "section", steps)
        source = (section - steps) % sections
        routed = jnp.where(image_of[0, source] == section, moved, routed)
    vision_grad = routed.reshape(1, 1, slot_rows, part_width)

    inner = (((0,), (0,)), ((), ()))
    grad_blocks = {}
    for code in key_blocks:
        piece = columns_of(image, (dp_index ^ code) * block_rows, block_rows)
        key_part = lax.dot_general(piece, key_flat, inner, preferred_element_type=jnp.float32)
        value_part = lax.dot_general(piece, value_flat, inner, preferred_element_type=jnp.float32)
        grad_blocks[code] = jnp.concatenate(
            [key_part.astype(jnp.bfloat16), value_part.astype(jnp.bfloat16)], axis=1
        )
    both_grads = scatter_blocks(grad_blocks, "dp").astype(jnp.bfloat16)
    key_weight_grad = both_grads[:, :width_k][None]
    value_weight_grad = both_grads[:, width_k:][None]
    return (gated_context, vision_grad, key_weight_grad, value_weight_grad)


def solution(mesh):
    return jax.shard_map(
        per_device,
        mesh=mesh,
        in_specs=(
            P("dp", "section", None, "mp"),
            P("dp", "section", None, "mp"),
            P("dp", None),
            P("dp", "section"),
            P("dp", None),
            P("section", None),
            P("section", "dp", "mp"),
            P("section", "dp", "mp"),
            P("section", "dp", "mp"),
            P("section", None),
            P("section", None),
            P("section"),
            P("dp", "section", None, "mp"),
        ),
        out_specs=(
            P("dp", "section", None, "mp"),
            P("dp", "section", None, "mp"),
            P("section", "dp", "mp"),
            P("section", "dp", "mp"),
        ),
        check_vma=False,
    )
```

```python
import jax
import jax.numpy as jnp
from jax import lax
from jax.sharding import PartitionSpec as P

HD = 128
TILE_ROWS = 64


def shifted(value, axis, steps):
    count = lax.axis_size(axis)
    pairs = [(source, (source + steps) % count) for source in range(count)]
    return lax.ppermute(value, axis, pairs)


def swapped(value, axis, mask):
    count = lax.axis_size(axis)
    pairs = [(source, source ^ mask) for source in range(count)]
    return lax.ppermute(value, axis, pairs)


def bit_order(count, high_first):
    bits = []
    step = 1
    while step < count:
        bits.append(step)
        step *= 2
    return bits[::-1] if high_first else bits


def gather_blocks(block, axis):
    count = lax.axis_size(axis)
    held = {0: block}
    for mask in bit_order(count, True):
        codes = sorted(held)
        arrived = swapped(jnp.stack([held[c] for c in codes]), axis, mask)
        for position, code in enumerate(codes):
            held[code ^ mask] = arrived[position]
    return held


def gather_groups(block, axis):
    count = lax.axis_size(axis)
    codes = [0]
    stack = block[None]
    groups = [(codes, stack)]
    for mask in bit_order(count, True):
        arrived = swapped(stack, axis, mask)
        moved = [code ^ mask for code in codes]
        groups = [(codes, stack), (moved, arrived)]
        stack = jnp.concatenate([stack, arrived], axis=0)
        codes = codes + moved
    return groups


def code_slices(values, index, codes, width):
    pieces = [lax.dynamic_slice_in_dim(values, (index ^ code) * width, width, axis=1) for code in codes]
    return pieces[0] if len(pieces) == 1 else jnp.concatenate(pieces, axis=1)


def scatter_blocks(by_code, axis):
    count = lax.axis_size(axis)
    held = {code: value.astype(jnp.float32) for code, value in by_code.items()}
    for mask in bit_order(count, False):
        sent = sorted(c for c in held if c & mask)
        kept = [c ^ mask for c in sent]
        arrived = swapped(jnp.stack([held[c].astype(jnp.bfloat16) for c in sent]), axis, mask)
        held = {c: held[c] + arrived[position].astype(jnp.float32) for position, c in enumerate(kept)}
    return held[0]


def norm_rows(values, gain):
    values = values.astype(jnp.float32)
    scaled = values * lax.rsqrt(jnp.mean(values * values, axis=-1, keepdims=True) + 1e-05)
    return scaled * gain


def rounded(values):
    return lax.optimization_barrier(values.astype(jnp.bfloat16)).astype(jnp.float32)


def attend(queries, keys_raw, values_raw, key_norm, usable, present, gate_value):
    keys = rounded(norm_rows(keys_raw, key_norm))
    values = rounded(values_raw)
    text_rows, heads, depth = queries.shape
    groups = keys.shape[1]
    grouped = queries.astype(jnp.float32).reshape(text_rows, groups, heads // groups, depth)
    scores = jnp.einsum("tgjd,vgd->gjtv", grouped, keys) * depth ** (-0.5)
    scores = jnp.where(usable[None, None, None, :], scores, -1e30)
    highest = lax.stop_gradient(jnp.max(scores, axis=-1, keepdims=True))
    weights = jnp.exp(scores - highest)
    probs = rounded(weights / jnp.sum(weights, axis=-1, keepdims=True))
    context = jnp.einsum("gjtv,vgd->tgjd", probs, values).reshape(text_rows, heads * depth)
    return jnp.where(present[:, None], jnp.tanh(gate_value) * context, 0.0)


def columns_of(values, start, width):
    return lax.dynamic_slice_in_dim(values, start, width, axis=1)


def per_device(
    text_in,
    vision,
    tile_counts,
    lengths,
    image_of,
    norm_gain,
    query_weight,
    key_weight,
    value_weight,
    query_gain,
    key_gain,
    cross_gate,
    context_grad,
):
    sections = lax.axis_size("section")
    section = lax.axis_index("section")
    dp_index = lax.axis_index("dp")
    block_rows = query_weight.shape[1]

    query_groups = gather_groups(query_weight[0], "dp")
    key_blocks = gather_blocks(key_weight[0], "dp")
    value_blocks = gather_blocks(value_weight[0], "dp")

    slot_rows = vision.shape[2]
    part_width = vision.shape[3]
    wanted = image_of[0, section]
    image_part = vision[0, 0]
    for steps in range(1, sections):
        moved = shifted(vision, "section", steps)[0, 0]
        image_part = jnp.where((section - steps) % sections == wanted, moved, image_part)
    image = lax.all_gather(image_part, "mp", axis=1, tiled=True)

    width_k = key_weight.shape[2]
    keys_raw = None
    values_raw = None
    for code in key_blocks:
        piece = columns_of(image, (dp_index ^ code) * block_rows, block_rows)
        key_part = jnp.dot(piece, key_blocks[code], preferred_element_type=jnp.float32)
        value_part = jnp.dot(piece, value_blocks[code], preferred_element_type=jnp.float32)
        keys_raw = key_part if keys_raw is None else keys_raw + key_part
        values_raw = value_part if values_raw is None else values_raw + value_part
    keys_raw = keys_raw.reshape(slot_rows, width_k // HD, HD)
    values_raw = values_raw.reshape(slot_rows, width_k // HD, HD)
    usable = jnp.arange(slot_rows) < tile_counts[0, wanted] * TILE_ROWS

    arrived = shifted(text_in, "section", 1)
    text_rows = text_in.shape[2]
    width_q = query_weight.shape[2]
    chunks = 2 if text_rows % 16 == 0 else 1
    rows = text_rows // chunks
    contexts = []
    key_back = None
    value_back = None
    gathered = [
        lax.all_gather(arrived[:, :, chunk * rows : (chunk + 1) * rows], "mp", axis=3, tiled=True)
        for chunk in range(chunks)
    ]
    for chunk in range(chunks):
        lower = chunk * rows
        full_text = gathered[chunk][0, 0]
        normed = norm_rows(full_text, norm_gain[0]).astype(jnp.bfloat16)
        query_raw = None
        for codes, stack in query_groups:
            part = jnp.dot(
                code_slices(normed, dp_index, codes, block_rows),
                stack.reshape(stack.shape[0] * stack.shape[1], stack.shape[2]),
                preferred_element_type=jnp.float32,
            )
            query_raw = part if query_raw is None else query_raw + part
        queries = norm_rows(query_raw.reshape(rows, width_q // HD, HD), query_gain[0]).astype(
            jnp.bfloat16
        )
        present = lower + jnp.arange(rows) < lengths[0, 0]

        def forward(keys_in, values_in):
            return attend(queries, keys_in, values_in, key_gain[0], usable, present, cross_gate[0])

        context, pullback = jax.vjp(forward, keys_raw, values_raw)
        contexts.append(context.astype(jnp.bfloat16))
        key_part, value_part = pullback(context_grad[0, 0, lower : lower + rows].astype(jnp.float32))
        key_back = key_part if key_back is None else key_back + key_part
        value_back = value_part if value_back is None else value_back + value_part
        if chunk + 1 < chunks:
            gathered[chunk + 1], key_back, value_back = lax.optimization_barrier(
                (gathered[chunk + 1], key_back, value_back)
            )
    gated_context = jnp.concatenate(contexts, axis=0).reshape(1, 1, text_rows, width_q)
    key_flat = key_back.reshape(slot_rows, width_k).astype(jnp.bfloat16)
    value_flat = value_back.reshape(slot_rows, width_k).astype(jnp.bfloat16)

    contract = (((1,), (1,)), ((), ()))
    partial_sum = jnp.zeros((slot_rows, image.shape[1]), jnp.bfloat16)
    for code in key_blocks:
        term = lax.dot_general(key_flat, key_blocks[code], contract, preferred_element_type=jnp.float32)
        term = term + lax.dot_general(
            value_flat, value_blocks[code], contract, preferred_element_type=jnp.float32
        )
        partial_sum = lax.dynamic_update_slice_in_dim(
            partial_sum, term.astype(jnp.bfloat16), (dp_index ^ code) * block_rows, axis=1
        )
    summed = lax.psum_scatter(partial_sum, "mp", scatter_dimension=1, tiled=True)

    routed = summed
    for steps in range(1, sections):
        moved = shifted(summed, "section", steps)
        source = (section - steps) % sections
        routed = jnp.where(image_of[0, source] == section, moved, routed)
    vision_grad = routed.reshape(1, 1, slot_rows, part_width)

    inner = (((0,), (0,)), ((), ()))
    grad_blocks = {}
    for code in key_blocks:
        piece = columns_of(image, (dp_index ^ code) * block_rows, block_rows)
        key_part = lax.dot_general(piece, key_flat, inner, preferred_element_type=jnp.float32)
        value_part = lax.dot_general(piece, value_flat, inner, preferred_element_type=jnp.float32)
        grad_blocks[code] = jnp.concatenate(
            [key_part.astype(jnp.bfloat16), value_part.astype(jnp.bfloat16)], axis=1
        )
    both_grads = scatter_blocks(grad_blocks, "dp").astype(jnp.bfloat16)
    key_weight_grad = both_grads[:, :width_k][None]
    value_weight_grad = both_grads[:, width_k:][None]
    return (gated_context, vision_grad, key_weight_grad, value_weight_grad)


def solution(mesh):
    return jax.shard_map(
        per_device,
        mesh=mesh,
        in_specs=(
            P("dp", "section", None, "mp"),
            P("dp", "section", None, "mp"),
            P("dp", None),
            P("dp", "section"),
            P("dp", None),
            P("section", None),
            P("section", "dp", "mp"),
            P("section", "dp", "mp"),
            P("section", "dp", "mp"),
            P("section", None),
            P("section", None),
            P("section"),
            P("dp", "section", None, "mp"),
        ),
        out_specs=(
            P("dp", "section", None, "mp"),
            P("dp", "section", None, "mp"),
            P("section", "dp", "mp"),
            P("section", "dp", "mp"),
        ),
        check_vma=False,
    )
```

```python
import jax
import jax.numpy as jnp
from jax import lax
from jax.sharding import PartitionSpec as P

HD = 128
TILE_ROWS = 64


def shifted(value, axis, steps):
    count = lax.axis_size(axis)
    pairs = [(source, (source + steps) % count) for source in range(count)]
    return lax.ppermute(value, axis, pairs)


def swapped(value, axis, mask):
    count = lax.axis_size(axis)
    pairs = [(source, source ^ mask) for source in range(count)]
    return lax.ppermute(value, axis, pairs)


def bit_order(count, high_first):
    bits = []
    step = 1
    while step < count:
        bits.append(step)
        step *= 2
    return bits[::-1] if high_first else bits


def gather_blocks(block, axis):
    count = lax.axis_size(axis)
    held = {0: block}
    for mask in bit_order(count, True):
        codes = sorted(held)
        arrived = swapped(jnp.stack([held[c] for c in codes]), axis, mask)
        for position, code in enumerate(codes):
            held[code ^ mask] = arrived[position]
    return held


def scatter_blocks(by_code, axis):
    count = lax.axis_size(axis)
    held = {code: value.astype(jnp.float32) for code, value in by_code.items()}
    for mask in bit_order(count, False):
        sent = sorted(c for c in held if c & mask)
        kept = [c ^ mask for c in sent]
        arrived = swapped(jnp.stack([held[c].astype(jnp.bfloat16) for c in sent]), axis, mask)
        held = {c: held[c] + arrived[position].astype(jnp.float32) for position, c in enumerate(kept)}
    return held[0]


def norm_rows(values, gain):
    values = values.astype(jnp.float32)
    scaled = values * lax.rsqrt(jnp.mean(values * values, axis=-1, keepdims=True) + 1e-05)
    return scaled * gain


def rounded(values):
    return lax.optimization_barrier(values.astype(jnp.bfloat16)).astype(jnp.float32)


def prepare(keys_raw, values_raw, key_norm):
    return rounded(norm_rows(keys_raw, key_norm)), rounded(values_raw)


def attend(queries, keys, values, usable, present, gate_value):
    text_rows, heads, depth = queries.shape
    groups = keys.shape[1]
    grouped = queries.astype(jnp.float32).reshape(text_rows, groups, heads // groups, depth)
    scores = jnp.einsum("tgjd,vgd->gjtv", grouped, keys) * depth ** (-0.5)
    scores = jnp.where(usable[None, None, None, :], scores, -1e30)
    highest = lax.stop_gradient(jnp.max(scores, axis=-1, keepdims=True))
    weights = jnp.exp(scores - highest)
    probs = rounded(weights / jnp.sum(weights, axis=-1, keepdims=True))
    context = jnp.einsum("gjtv,vgd->tgjd", probs, values).reshape(text_rows, heads * depth)
    return jnp.where(present[:, None], jnp.tanh(gate_value) * context, 0.0)


def columns_of(values, start, width):
    return lax.dynamic_slice_in_dim(values, start, width, axis=1)


def per_device(
    text_in,
    vision,
    tile_counts,
    lengths,
    image_of,
    norm_gain,
    query_weight,
    key_weight,
    value_weight,
    query_gain,
    key_gain,
    cross_gate,
    context_grad,
):
    sections = lax.axis_size("section")
    section = lax.axis_index("section")
    dp_index = lax.axis_index("dp")
    block_rows = query_weight.shape[1]

    query_blocks = gather_blocks(query_weight[0], "dp")
    key_blocks = gather_blocks(key_weight[0], "dp")
    value_blocks = gather_blocks(value_weight[0], "dp")

    slot_rows = vision.shape[2]
    part_width = vision.shape[3]
    wanted = image_of[0, section]
    image_part = vision[0, 0]
    for steps in range(1, sections):
        moved = shifted(vision, "section", steps)[0, 0]
        image_part = jnp.where((section - steps) % sections == wanted, moved, image_part)
    image = lax.all_gather(image_part, "mp", axis=1, tiled=True)

    width_k = key_weight.shape[2]
    keys_raw = None
    values_raw = None
    for code in key_blocks:
        piece = columns_of(image, (dp_index ^ code) * block_rows, block_rows)
        key_part = jnp.dot(piece, key_blocks[code], preferred_element_type=jnp.float32)
        value_part = jnp.dot(piece, value_blocks[code], preferred_element_type=jnp.float32)
        keys_raw = key_part if keys_raw is None else keys_raw + key_part
        values_raw = value_part if values_raw is None else values_raw + value_part
    keys_raw = keys_raw.reshape(slot_rows, width_k // HD, HD)
    values_raw = values_raw.reshape(slot_rows, width_k // HD, HD)
    usable = jnp.arange(slot_rows) < tile_counts[0, wanted] * TILE_ROWS
    (keys, values), prepare_back = jax.vjp(
        lambda keys_in, values_in: prepare(keys_in, values_in, key_gain[0]), keys_raw, values_raw
    )

    arrived = shifted(text_in, "section", 1)
    text_rows = text_in.shape[2]
    width_q = query_weight.shape[2]
    chunks = 2 if text_rows % 16 == 0 else 1
    rows = text_rows // chunks
    contexts = []
    key_back = None
    value_back = None
    gathered = [
        lax.all_gather(arrived[:, :, chunk * rows : (chunk + 1) * rows], "mp", axis=3, tiled=True)
        for chunk in range(chunks)
    ]
    for chunk in range(chunks):
        lower = chunk * rows
        full_text = gathered[chunk][0, 0]
        normed = norm_rows(full_text, norm_gain[0]).astype(jnp.bfloat16)
        query_raw = None
        for code, block in query_blocks.items():
            part = jnp.dot(
                columns_of(normed, (dp_index ^ code) * block_rows, block_rows),
                block,
                preferred_element_type=jnp.float32,
            )
            query_raw = part if query_raw is None else query_raw + part
        queries = norm_rows(query_raw.reshape(rows, width_q // HD, HD), query_gain[0]).astype(
            jnp.bfloat16
        )
        present = lower + jnp.arange(rows) < lengths[0, 0]

        def forward(keys_in, values_in):
            return attend(queries, keys_in, values_in, usable, present, cross_gate[0])

        context, pullback = jax.vjp(forward, keys, values)
        contexts.append(context.astype(jnp.bfloat16))
        key_part, value_part = pullback(context_grad[0, 0, lower : lower + rows].astype(jnp.float32))
        key_back = key_part if key_back is None else key_back + key_part
        value_back = value_part if value_back is None else value_back + value_part
        if chunk + 1 < chunks:
            gathered[chunk + 1], key_back, value_back = lax.optimization_barrier(
                (gathered[chunk + 1], key_back, value_back)
            )
    gated_context = jnp.concatenate(contexts, axis=0).reshape(1, 1, text_rows, width_q)
    key_back, value_back = prepare_back((key_back, value_back))
    key_flat = key_back.reshape(slot_rows, width_k).astype(jnp.bfloat16)
    value_flat = value_back.reshape(slot_rows, width_k).astype(jnp.bfloat16)

    contract = (((1,), (1,)), ((), ()))
    partial_sum = jnp.zeros((slot_rows, image.shape[1]), jnp.bfloat16)
    for code in key_blocks:
        term = lax.dot_general(key_flat, key_blocks[code], contract, preferred_element_type=jnp.float32)
        term = term + lax.dot_general(
            value_flat, value_blocks[code], contract, preferred_element_type=jnp.float32
        )
        partial_sum = lax.dynamic_update_slice_in_dim(
            partial_sum, term.astype(jnp.bfloat16), (dp_index ^ code) * block_rows, axis=1
        )
    summed = lax.psum_scatter(partial_sum, "mp", scatter_dimension=1, tiled=True)

    routed = summed
    for steps in range(1, sections):
        moved = shifted(summed, "section", steps)
        source = (section - steps) % sections
        routed = jnp.where(image_of[0, source] == section, moved, routed)
    vision_grad = routed.reshape(1, 1, slot_rows, part_width)

    inner = (((0,), (0,)), ((), ()))
    grad_blocks = {}
    for code in key_blocks:
        piece = columns_of(image, (dp_index ^ code) * block_rows, block_rows)
        key_part = lax.dot_general(piece, key_flat, inner, preferred_element_type=jnp.float32)
        value_part = lax.dot_general(piece, value_flat, inner, preferred_element_type=jnp.float32)
        grad_blocks[code] = jnp.concatenate(
            [key_part.astype(jnp.bfloat16), value_part.astype(jnp.bfloat16)], axis=1
        )
    both_grads = scatter_blocks(grad_blocks, "dp").astype(jnp.bfloat16)
    key_weight_grad = both_grads[:, :width_k][None]
    value_weight_grad = both_grads[:, width_k:][None]
    return (gated_context, vision_grad, key_weight_grad, value_weight_grad)


def solution(mesh):
    return jax.shard_map(
        per_device,
        mesh=mesh,
        in_specs=(
            P("dp", "section", None, "mp"),
            P("dp", "section", None, "mp"),
            P("dp", None),
            P("dp", "section"),
            P("dp", None),
            P("section", None),
            P("section", "dp", "mp"),
            P("section", "dp", "mp"),
            P("section", "dp", "mp"),
            P("section", None),
            P("section", None),
            P("section"),
            P("dp", "section", None, "mp"),
        ),
        out_specs=(
            P("dp", "section", None, "mp"),
            P("dp", "section", None, "mp"),
            P("section", "dp", "mp"),
            P("section", "dp", "mp"),
        ),
        check_vma=False,
    )
```

```python
import jax
import jax.numpy as jnp
from jax import lax
from jax.sharding import PartitionSpec as P

HD = 128
TILE_ROWS = 64


def shifted(value, axis, steps):
    count = lax.axis_size(axis)
    pairs = [(source, (source + steps) % count) for source in range(count)]
    return lax.ppermute(value, axis, pairs)


def swapped(value, axis, mask):
    count = lax.axis_size(axis)
    pairs = [(source, source ^ mask) for source in range(count)]
    return lax.ppermute(value, axis, pairs)


def bit_order(count, high_first):
    bits = []
    step = 1
    while step < count:
        bits.append(step)
        step *= 2
    return bits[::-1] if high_first else bits


def gather_blocks(block, axis):
    count = lax.axis_size(axis)
    held = {0: block}
    for mask in bit_order(count, True):
        codes = sorted(held)
        arrived = swapped(jnp.stack([held[c] for c in codes]), axis, mask)
        for position, code in enumerate(codes):
            held[code ^ mask] = arrived[position]
    return held


def scatter_blocks(by_code, axis):
    count = lax.axis_size(axis)
    held = {code: value.astype(jnp.float32) for code, value in by_code.items()}
    for mask in bit_order(count, False):
        sent = sorted(c for c in held if c & mask)
        kept = [c ^ mask for c in sent]
        arrived = swapped(jnp.stack([held[c].astype(jnp.bfloat16) for c in sent]), axis, mask)
        held = {c: held[c] + arrived[position].astype(jnp.float32) for position, c in enumerate(kept)}
    return held[0]


def norm_rows(values, gain):
    values = values.astype(jnp.float32)
    scaled = values * lax.rsqrt(jnp.mean(values * values, axis=-1, keepdims=True) + 1e-05)
    return scaled * gain


def rounded(values):
    return lax.optimization_barrier(values.astype(jnp.bfloat16)).astype(jnp.float32)


def prepare(keys_raw, values_raw, key_norm):
    return rounded(norm_rows(keys_raw, key_norm)), rounded(values_raw)


def attend(queries, keys, values, usable, present, gate_value):
    text_rows, heads, depth = queries.shape
    groups = keys.shape[1]
    grouped = queries.astype(jnp.float32).reshape(text_rows, groups, heads // groups, depth)
    scores = jnp.einsum("tgjd,vgd->gjtv", grouped, keys) * depth ** (-0.5)
    scores = jnp.where(usable[None, None, None, :], scores, -1e30)
    highest = lax.stop_gradient(jnp.max(scores, axis=-1, keepdims=True))
    weights = jnp.exp(scores - highest)
    probs = rounded(weights / jnp.sum(weights, axis=-1, keepdims=True))
    context = jnp.einsum("gjtv,vgd->tgjd", probs, values).reshape(text_rows, heads * depth)
    return jnp.where(present[:, None], jnp.tanh(gate_value) * context, 0.0)


def columns_of(values, start, width):
    return lax.dynamic_slice_in_dim(values, start, width, axis=1)


def per_device(
    text_in,
    vision,
    tile_counts,
    lengths,
    image_of,
    norm_gain,
    query_weight,
    key_weight,
    value_weight,
    query_gain,
    key_gain,
    cross_gate,
    context_grad,
):
    sections = lax.axis_size("section")
    section = lax.axis_index("section")
    dp_index = lax.axis_index("dp")
    block_rows = query_weight.shape[1]

    query_blocks = gather_blocks(query_weight[0], "dp")
    key_blocks = gather_blocks(key_weight[0], "dp")
    value_blocks = gather_blocks(value_weight[0], "dp")

    slot_rows = vision.shape[2]
    part_width = vision.shape[3]
    wanted = image_of[0, section]
    image_part = vision[0, 0]
    for steps in range(1, sections):
        moved = shifted(vision, "section", steps)[0, 0]
        image_part = jnp.where((section - steps) % sections == wanted, moved, image_part)
    image = lax.all_gather(image_part, "mp", axis=1, tiled=True)

    width_k = key_weight.shape[2]
    keys_raw = None
    values_raw = None
    for code in key_blocks:
        piece = columns_of(image, (dp_index ^ code) * block_rows, block_rows)
        key_part = jnp.dot(piece, key_blocks[code], preferred_element_type=jnp.float32)
        value_part = jnp.dot(piece, value_blocks[code], preferred_element_type=jnp.float32)
        keys_raw = key_part if keys_raw is None else keys_raw + key_part
        values_raw = value_part if values_raw is None else values_raw + value_part
    keys_raw = keys_raw.reshape(slot_rows, width_k // HD, HD)
    values_raw = values_raw.reshape(slot_rows, width_k // HD, HD)
    usable = jnp.arange(slot_rows) < tile_counts[0, wanted] * TILE_ROWS
    (keys, values), prepare_back = jax.vjp(
        lambda keys_in, values_in: prepare(keys_in, values_in, key_gain[0]), keys_raw, values_raw
    )

    arrived = shifted(text_in, "section", 1)
    text_rows = text_in.shape[2]
    width_q = query_weight.shape[2]
    chunks = 2 if text_rows % 16 == 0 else 1
    rows = text_rows // chunks
    contexts = []
    key_back = None
    value_back = None
    gathered = [
        lax.all_gather(arrived[:, :, chunk * rows : (chunk + 1) * rows], "mp", axis=3, tiled=True)
        for chunk in range(chunks)
    ]
    for chunk in range(chunks):
        lower = chunk * rows
        full_text = gathered[chunk][0, 0]
        normed = norm_rows(full_text, norm_gain[0]).astype(jnp.bfloat16)
        query_raw = None
        for code, block in query_blocks.items():
            part = jnp.dot(
                columns_of(normed, (dp_index ^ code) * block_rows, block_rows),
                block,
                preferred_element_type=jnp.float32,
            )
            query_raw = part if query_raw is None else query_raw + part
        queries = norm_rows(query_raw.reshape(rows, width_q // HD, HD), query_gain[0]).astype(
            jnp.bfloat16
        )
        present = lower + jnp.arange(rows) < lengths[0, 0]

        def forward(keys_in, values_in):
            return attend(queries, keys_in, values_in, usable, present, cross_gate[0])

        context, pullback = jax.vjp(forward, keys, values)
        contexts.append(context.astype(jnp.bfloat16))
        key_part, value_part = pullback(context_grad[0, 0, lower : lower + rows].astype(jnp.float32))
        key_back = key_part if key_back is None else key_back + key_part
        value_back = value_part if value_back is None else value_back + value_part
        if chunk + 1 < chunks:
            gathered[chunk + 1], key_back, value_back = lax.optimization_barrier(
                (gathered[chunk + 1], key_back, value_back)
            )
    gated_context = jnp.concatenate(contexts, axis=0).reshape(1, 1, text_rows, width_q)
    key_back, value_back = prepare_back((key_back, value_back))
    key_flat = key_back.reshape(slot_rows, width_k).astype(jnp.bfloat16)
    value_flat = value_back.reshape(slot_rows, width_k).astype(jnp.bfloat16)

    contract = (((1,), (1,)), ((), ()))
    dp_count = lax.axis_size("dp")
    terms = []
    for code in range(dp_count):
        term = lax.dot_general(key_flat, key_blocks[code], contract, preferred_element_type=jnp.float32)
        term = term + lax.dot_general(
            value_flat, value_blocks[code], contract, preferred_element_type=jnp.float32
        )
        terms.append(term.astype(jnp.bfloat16))
    in_code_order = jnp.concatenate(terms, axis=1)
    partial_sum = jnp.concatenate(
        [columns_of(in_code_order, (dp_index ^ block) * block_rows, block_rows) for block in range(dp_count)],
        axis=1,
    )
    summed = lax.psum_scatter(partial_sum, "mp", scatter_dimension=1, tiled=True)

    routed = summed
    for steps in range(1, sections):
        moved = shifted(summed, "section", steps)
        source = (section - steps) % sections
        routed = jnp.where(image_of[0, source] == section, moved, routed)
    vision_grad = routed.reshape(1, 1, slot_rows, part_width)

    inner = (((0,), (0,)), ((), ()))
    grad_blocks = {}
    for code in key_blocks:
        piece = columns_of(image, (dp_index ^ code) * block_rows, block_rows)
        key_part = lax.dot_general(piece, key_flat, inner, preferred_element_type=jnp.float32)
        value_part = lax.dot_general(piece, value_flat, inner, preferred_element_type=jnp.float32)
        grad_blocks[code] = jnp.concatenate(
            [key_part.astype(jnp.bfloat16), value_part.astype(jnp.bfloat16)], axis=1
        )
    both_grads = scatter_blocks(grad_blocks, "dp").astype(jnp.bfloat16)
    key_weight_grad = both_grads[:, :width_k][None]
    value_weight_grad = both_grads[:, width_k:][None]
    return (gated_context, vision_grad, key_weight_grad, value_weight_grad)


def solution(mesh):
    return jax.shard_map(
        per_device,
        mesh=mesh,
        in_specs=(
            P("dp", "section", None, "mp"),
            P("dp", "section", None, "mp"),
            P("dp", None),
            P("dp", "section"),
            P("dp", None),
            P("section", None),
            P("section", "dp", "mp"),
            P("section", "dp", "mp"),
            P("section", "dp", "mp"),
            P("section", None),
            P("section", None),
            P("section"),
            P("dp", "section", None, "mp"),
        ),
        out_specs=(
            P("dp", "section", None, "mp"),
            P("dp", "section", None, "mp"),
            P("section", "dp", "mp"),
            P("section", "dp", "mp"),
        ),
        check_vma=False,
    )
```

```python
import jax
import jax.numpy as jnp
from jax import lax
from jax.sharding import PartitionSpec as P

HD = 128
TILE_ROWS = 64


def shifted(value, axis, steps):
    count = lax.axis_size(axis)
    pairs = [(source, (source + steps) % count) for source in range(count)]
    return lax.ppermute(value, axis, pairs)


def swapped(value, axis, mask):
    count = lax.axis_size(axis)
    pairs = [(source, source ^ mask) for source in range(count)]
    return lax.ppermute(value, axis, pairs)


def bit_order(count, high_first):
    bits = []
    step = 1
    while step < count:
        bits.append(step)
        step *= 2
    return bits[::-1] if high_first else bits


def gather_blocks(block, axis):
    count = lax.axis_size(axis)
    held = {0: block}
    for mask in bit_order(count, True):
        codes = sorted(held)
        arrived = swapped(jnp.stack([held[c] for c in codes]), axis, mask)
        for position, code in enumerate(codes):
            held[code ^ mask] = arrived[position]
    return held


def scatter_blocks(by_code, axis):
    count = lax.axis_size(axis)
    held = {code: value.astype(jnp.float32) for code, value in by_code.items()}
    for mask in bit_order(count, False):
        sent = sorted(c for c in held if c & mask)
        kept = [c ^ mask for c in sent]
        arrived = swapped(jnp.stack([held[c].astype(jnp.bfloat16) for c in sent]), axis, mask)
        held = {c: held[c] + arrived[position].astype(jnp.float32) for position, c in enumerate(kept)}
    return held[0]


def norm_rows(values, gain):
    values = values.astype(jnp.float32)
    scaled = values * lax.rsqrt(jnp.mean(values * values, axis=-1, keepdims=True) + 1e-05)
    return scaled * gain


def rounded(values):
    return values.astype(jnp.bfloat16).astype(jnp.float32)


def prepare(keys_raw, values_raw, key_norm):
    return rounded(norm_rows(keys_raw, key_norm)), rounded(values_raw)


def attend(queries, keys, values, usable, present, gate_value):
    text_rows, heads, depth = queries.shape
    groups = keys.shape[1]
    grouped = queries.astype(jnp.float32).reshape(text_rows, groups, heads // groups, depth)
    scores = jnp.einsum("tgjd,vgd->gjtv", grouped, keys) * depth ** (-0.5)
    scores = jnp.where(usable[None, None, None, :], scores, -1e30)
    highest = lax.stop_gradient(jnp.max(scores, axis=-1, keepdims=True))
    weights = jnp.exp(scores - highest)
    probs = rounded(weights / jnp.sum(weights, axis=-1, keepdims=True))
    context = jnp.einsum("gjtv,vgd->tgjd", probs, values).reshape(text_rows, heads * depth)
    return jnp.where(present[:, None], jnp.tanh(gate_value) * context, 0.0)


def columns_of(values, start, width):
    return lax.dynamic_slice_in_dim(values, start, width, axis=1)


def per_device(
    text_in,
    vision,
    tile_counts,
    lengths,
    image_of,
    norm_gain,
    query_weight,
    key_weight,
    value_weight,
    query_gain,
    key_gain,
    cross_gate,
    context_grad,
):
    sections = lax.axis_size("section")
    section = lax.axis_index("section")
    dp_index = lax.axis_index("dp")
    block_rows = query_weight.shape[1]

    query_blocks = gather_blocks(query_weight[0], "dp")
    key_blocks = gather_blocks(key_weight[0], "dp")
    value_blocks = gather_blocks(value_weight[0], "dp")

    slot_rows = vision.shape[2]
    part_width = vision.shape[3]
    wanted = image_of[0, section]
    image_part = vision[0, 0]
    for steps in range(1, sections):
        moved = shifted(vision, "section", steps)[0, 0]
        image_part = jnp.where((section - steps) % sections == wanted, moved, image_part)
    image = lax.all_gather(image_part, "mp", axis=1, tiled=True)

    width_k = key_weight.shape[2]
    keys_raw = None
    values_raw = None
    for code in key_blocks:
        piece = columns_of(image, (dp_index ^ code) * block_rows, block_rows)
        key_part = jnp.dot(piece, key_blocks[code], preferred_element_type=jnp.float32)
        value_part = jnp.dot(piece, value_blocks[code], preferred_element_type=jnp.float32)
        keys_raw = key_part if keys_raw is None else keys_raw + key_part
        values_raw = value_part if values_raw is None else values_raw + value_part
    keys_raw = keys_raw.reshape(slot_rows, width_k // HD, HD)
    values_raw = values_raw.reshape(slot_rows, width_k // HD, HD)
    usable = jnp.arange(slot_rows) < tile_counts[0, wanted] * TILE_ROWS
    (keys, values), prepare_back = jax.vjp(
        lambda keys_in, values_in: prepare(keys_in, values_in, key_gain[0]), keys_raw, values_raw
    )

    arrived = shifted(text_in, "section", 1)
    text_rows = text_in.shape[2]
    width_q = query_weight.shape[2]
    chunks = 2 if text_rows % 16 == 0 else 1
    rows = text_rows // chunks
    contexts = []
    key_back = None
    value_back = None
    gathered = [
        lax.all_gather(arrived[:, :, chunk * rows : (chunk + 1) * rows], "mp", axis=3, tiled=True)
        for chunk in range(chunks)
    ]
    for chunk in range(chunks):
        lower = chunk * rows
        full_text = gathered[chunk][0, 0]
        normed = norm_rows(full_text, norm_gain[0]).astype(jnp.bfloat16)
        query_raw = None
        for code, block in query_blocks.items():
            part = jnp.dot(
                columns_of(normed, (dp_index ^ code) * block_rows, block_rows),
                block,
                preferred_element_type=jnp.float32,
            )
            query_raw = part if query_raw is None else query_raw + part
        queries = norm_rows(query_raw.reshape(rows, width_q // HD, HD), query_gain[0]).astype(
            jnp.bfloat16
        )
        present = lower + jnp.arange(rows) < lengths[0, 0]

        def forward(keys_in, values_in):
            return attend(queries, keys_in, values_in, usable, present, cross_gate[0])

        context, pullback = jax.vjp(forward, keys, values)
        contexts.append(context.astype(jnp.bfloat16))
        key_part, value_part = pullback(context_grad[0, 0, lower : lower + rows].astype(jnp.float32))
        key_back = key_part if key_back is None else key_back + key_part
        value_back = value_part if value_back is None else value_back + value_part
        if chunk + 1 < chunks:
            gathered[chunk + 1], key_back, value_back = lax.optimization_barrier(
                (gathered[chunk + 1], key_back, value_back)
            )
    gated_context = jnp.concatenate(contexts, axis=0).reshape(1, 1, text_rows, width_q)
    key_back, value_back = prepare_back((key_back, value_back))
    key_flat = key_back.reshape(slot_rows, width_k).astype(jnp.bfloat16)
    value_flat = value_back.reshape(slot_rows, width_k).astype(jnp.bfloat16)

    contract = (((1,), (1,)), ((), ()))
    dp_count = lax.axis_size("dp")
    terms = []
    for code in range(dp_count):
        term = lax.dot_general(key_flat, key_blocks[code], contract, preferred_element_type=jnp.float32)
        term = term + lax.dot_general(
            value_flat, value_blocks[code], contract, preferred_element_type=jnp.float32
        )
        terms.append(term.astype(jnp.bfloat16))
    in_code_order = jnp.concatenate(terms, axis=1)
    partial_sum = jnp.concatenate(
        [columns_of(in_code_order, (dp_index ^ block) * block_rows, block_rows) for block in range(dp_count)],
        axis=1,
    )
    summed = lax.psum_scatter(partial_sum, "mp", scatter_dimension=1, tiled=True)

    routed = summed
    for steps in range(1, sections):
        moved = shifted(summed, "section", steps)
        source = (section - steps) % sections
        routed = jnp.where(image_of[0, source] == section, moved, routed)
    vision_grad = routed.reshape(1, 1, slot_rows, part_width)

    inner = (((0,), (0,)), ((), ()))
    grad_blocks = {}
    for code in key_blocks:
        piece = columns_of(image, (dp_index ^ code) * block_rows, block_rows)
        key_part = lax.dot_general(piece, key_flat, inner, preferred_element_type=jnp.float32)
        value_part = lax.dot_general(piece, value_flat, inner, preferred_element_type=jnp.float32)
        grad_blocks[code] = jnp.concatenate(
            [key_part.astype(jnp.bfloat16), value_part.astype(jnp.bfloat16)], axis=1
        )
    both_grads = scatter_blocks(grad_blocks, "dp").astype(jnp.bfloat16)
    key_weight_grad = both_grads[:, :width_k][None]
    value_weight_grad = both_grads[:, width_k:][None]
    return (gated_context, vision_grad, key_weight_grad, value_weight_grad)


def solution(mesh):
    return jax.shard_map(
        per_device,
        mesh=mesh,
        in_specs=(
            P("dp", "section", None, "mp"),
            P("dp", "section", None, "mp"),
            P("dp", None),
            P("dp", "section"),
            P("dp", None),
            P("section", None),
            P("section", "dp", "mp"),
            P("section", "dp", "mp"),
            P("section", "dp", "mp"),
            P("section", None),
            P("section", None),
            P("section"),
            P("dp", "section", None, "mp"),
        ),
        out_specs=(
            P("dp", "section", None, "mp"),
            P("dp", "section", None, "mp"),
            P("section", "dp", "mp"),
            P("section", "dp", "mp"),
        ),
        check_vma=False,
    )
```
